32 devices in a mesh: row: 8 (over z, y), col: 4 (over x, core).
Axes of the slice: x: 2, y: 2, z: 4, core: 2. Of those that a mesh axis runs over, the one named last changes fastest.
Arguments:
- density: float32 [4, 256, 2048], P('col', 'row'), may hold values from 0.5 to 2
- momentum: float32 [3, 4, 256, 2048], P(None, 'col', 'row'), may hold values from -6 to 6
- energy: float32 [4, 256, 2048], P('col', 'row'), may hold values from 2 to 5
Outputs:
- tendency: float32 [5, 4, 256, 2048], P(None, 'col', 'row')
The draws below stay inside these ranges and needn't reach their ends.
All inputs are finite; a program needn't handle non-finite values.
Results may differ from the reference program's by a relative error of at most 0.000053.
Values sent between devices are 32-bit elements; how exact they have to be, the bound alone decides.
No kernel may reach another device: no remote copies, remote signals or barrier semaphores. Data moves between devices by JAX's collectives and lax.ppermute only.
A program may use at most 64 MiB of HBM per device.

```python
import jax
import jax.numpy as jnp
from jax import lax

NX = 2048
NY = 256
NZ = 4


def steps_of(own_key, dims, cuts, smallest, largest):
    factor_of = 1.0
    for dim, blocks in cuts:
        steps = jax.random.uniform(jax.random.fold_in(jax.random.fold_in(own_key, 6), dim), (blocks,), jnp.float32, smallest / len(cuts), largest / len(cuts))
        factor_of = factor_of * jnp.repeat(jnp.exp(steps), dims[dim] // blocks).reshape((-1,) + (1,) * (len(dims) - 1 - dim))
    return factor_of


def scatter_about(stream_key, extent, spread, bound, shards=(), kind=jnp.bfloat16):
    entries = spread * jax.random.normal(stream_key, extent, jnp.float32)
    if shards:
        entries = entries * steps_of(stream_key, extent, shards, -0.22, 0.18)
    return jnp.clip(entries, -bound, bound).astype(kind)


def setup_inputs(seed: int = 0) -> dict:
    seeds = jax.random.split(jax.random.key(seed), 4)
    density = jnp.clip(0.5 + 1.5 * jax.random.uniform(seeds[0], (NZ, NY, NX), jnp.float32) ** steps_of(seeds[0], (NZ, NY, NX), ((0, 4), (1, 8)), -0.2, 0.2), 0.5, 2.0)
    momentum = scatter_about(seeds[1], (3, NZ, NY, NX), 1.0, 6.0, ((1, 4), (2, 8)), jnp.float32)
    energy = jnp.clip(2.0 + 3.0 * jax.random.uniform(seeds[2], (NZ, NY, NX), jnp.float32) ** steps_of(seeds[2], (NZ, NY, NX), ((0, 4), (1, 8)), -0.2, 0.2), 2.0, 5.0)
    return dict(density=density, momentum=momentum, energy=energy)


def symbol(count):
    wave = 2.0 * jnp.pi * jnp.fft.rfftfreq(count)
    upper = (17.0 / 12.0) * jnp.sin(wave) + (101.0 / 300.0) * jnp.sin(2.0 * wave) + (1.0 / 300.0) * jnp.sin(3.0 * wave)
    lower = 1.0 + jnp.cos(wave) + 0.1 * jnp.cos(2.0 * wave)
    return 1j * upper / lower


def compact_last(field):
    count = field.shape[-1]
    spectrum = jnp.fft.rfft(field, axis=-1) * symbol(count)
    return jnp.fft.irfft(spectrum, n=count, axis=-1).astype(field.dtype)


def fluxes(density, momentum, energy):
    speed = momentum / density[None]
    pressure = 0.4 * (energy - 0.5 * jnp.sum(momentum * momentum, axis=0) / density)
    enthalpy = energy + pressure
    vel_x, vel_y = speed[0], speed[1]
    flux_x = jnp.stack([momentum[0], momentum[0] * vel_x + pressure, momentum[1] * vel_x, momentum[2] * vel_x, enthalpy * vel_x])
    flux_y = jnp.stack([momentum[1], momentum[0] * vel_y, momentum[1] * vel_y + pressure, momentum[2] * vel_y, enthalpy * vel_y])
    return flux_x, flux_y


def plane_tendency(inputs):
    density, momentum, energy = inputs
    flux_x, flux_y = fluxes(density, momentum, energy)
    derivative_x = compact_last(flux_x)
    derivative_y = jnp.swapaxes(compact_last(jnp.swapaxes(flux_y, 1, 2)), 1, 2)
    return -(derivative_x + derivative_y)


def reference(density, momentum, energy):
    planes = lax.map(plane_tendency, (density, jnp.moveaxis(momentum, 1, 0), energy))
    return jnp.moveaxis(planes, 0, 1)
```

```python
import jax
import jax.numpy as jnp
import numpy as np
from jax import lax
from jax.sharding import PartitionSpec as P


def operator_column(count):
    steps = np.arange(count)
    wave = 2.0 * np.pi * steps / count
    upper = (
        17.0 / 12.0 * np.sin(wave)
        + 101.0 / 300.0 * np.sin(2.0 * wave)
        + 1.0 / 300.0 * np.sin(3.0 * wave)
    )
    lower = 1.0 + np.cos(wave) + 0.1 * np.cos(2.0 * wave)
    ratio = upper / lower
    phase = 2.0 * np.pi * (steps[:, None] * steps[None, :] % count) / count
    return -np.sum(ratio[:, None] * np.sin(phase), axis=0) / count


def operator_table(count):
    column = operator_column(count)
    steps = np.arange(count)
    offsets = (steps[None, :] - steps[:, None]) % count
    return column[offsets].astype(np.float32)


def block_weights(count):
    table = operator_table(count)
    width = 128
    w_self = table[:width, :width]
    w_prev = table[:width, width : 2 * width]
    w_next = table[width : 2 * width, :width]
    return jnp.asarray(np.concatenate([w_prev, w_self, w_next], axis=1))


def compact_last(field):
    count = field.shape[-1]
    width = 128
    blocks = field.reshape(field.shape[:-1] + (count // width, width))
    parts = jnp.einsum(
        "...bj,jk->...bk", blocks, block_weights(count), precision=lax.Precision.HIGHEST
    )
    result = (
        jnp.roll(parts[..., :width], 1, axis=-2)
        + parts[..., width : 2 * width]
        + jnp.roll(parts[..., 2 * width :], -1, axis=-2)
    )
    return result.reshape(field.shape)


def column_basis(block, tol=1e-12):
    rest = block.copy()
    basis = []
    while len(basis) < block.shape[1]:
        norms = np.sqrt(np.sum(rest * rest, axis=0))
        pick = int(np.argmax(norms))
        if norms[pick] <= tol:
            break
        vec = rest[:, pick].copy()
        for _ in range(2):
            for q in basis:
                vec = vec - np.sum(q * vec) * q
        vec = vec / np.sqrt(np.sum(vec * vec))
        basis.append(vec)
        rest = rest - vec[:, None] * np.sum(vec[:, None] * rest, axis=0)[None, :]
    return basis


def y_operator(rows, groups):
    count = rows * groups
    column = operator_column(count)
    steps = np.arange(count)
    full = column[(steps[:, None] - steps[None, :]) % count]
    own = full[:rows, :rows].astype(np.float32)
    shifts = []
    for e in range(1, groups):
        block = full[:rows, rows * e : rows * (e + 1)]
        basis = column_basis(block)
        if not basis:
            continue
        q = np.stack(basis, axis=1)
        w = np.sum(q[:, :, None] * block[:, None, :], axis=0)
        shifts.append((e, q.astype(np.float32), w.astype(np.float32)))
    return own, shifts


def fluxes(density, momentum, energy):
    speed = momentum / density[None]
    pressure = 0.4 * (energy - 0.5 * jnp.sum(momentum * momentum, axis=0) / density)
    enthalpy = energy + pressure
    vel_x, vel_y = (speed[0], speed[1])
    flux_x = jnp.stack(
        [
            momentum[0],
            momentum[0] * vel_x + pressure,
            momentum[1] * vel_x,
            momentum[2] * vel_x,
            enthalpy * vel_x,
        ]
    )
    flux_y = jnp.stack(
        [
            momentum[1],
            momentum[0] * vel_y,
            momentum[1] * vel_y + pressure,
            momentum[2] * vel_y,
            enthalpy * vel_y,
        ]
    )
    return (flux_x, flux_y)


def make_local(groups):
    def local(density, momentum, energy):
        flux_x, flux_y = fluxes(density, momentum, energy)
        rows = flux_y.shape[2]
        own, shifts = y_operator(rows, groups)
        derivative_x = compact_last(flux_x)
        hi = lax.Precision.HIGHEST
        weights = jnp.asarray(np.concatenate([w for _, _, w in shifts], axis=0))
        moments = jnp.einsum("rq,fzqx->rfzx", weights, flux_y, precision=hi)
        received = []
        start = 0
        for e, q, w in shifts:
            part = moments[start : start + w.shape[0]]
            start += w.shape[0]
            perm = [(j, (j - e) % groups) for j in range(groups)]
            received.append(lax.ppermute(part, "row", perm))
        received = jnp.concatenate(received, axis=0)
        spread = jnp.asarray(np.concatenate([q for _, q, _ in shifts], axis=1))
        derivative_y = jnp.einsum("pq,fzqx->fzpx", jnp.asarray(own), flux_y, precision=hi)
        derivative_y = derivative_y + jnp.einsum(
            "pr,rfzx->fzpx", spread, received, precision=hi
        )
        return -(derivative_x + derivative_y)

    return local


def solution(mesh):
    in_specs = (P("col", "row", None), P(None, "col", "row", None), P("col", "row", None))
    out_specs = P(None, "col", "row", None)
    return jax.shard_map(
        make_local(mesh.shape["row"]),
        mesh=mesh,
        in_specs=in_specs,
        out_specs=out_specs,
        check_vma=False,
    )
```

```python
import jax
import jax.numpy as jnp
import numpy as np
from jax import lax
from jax.experimental import pallas as pl
from jax.experimental.pallas import tpu as pltpu
from jax.sharding import PartitionSpec as P


def operator_column(count):
    steps = np.arange(count)
    wave = 2.0 * np.pi * steps / count
    upper = (
        17.0 / 12.0 * np.sin(wave)
        + 101.0 / 300.0 * np.sin(2.0 * wave)
        + 1.0 / 300.0 * np.sin(3.0 * wave)
    )
    lower = 1.0 + np.cos(wave) + 0.1 * np.cos(2.0 * wave)
    ratio = upper / lower
    phase = 2.0 * np.pi * (steps[:, None] * steps[None, :] % count) / count
    return -np.sum(ratio[:, None] * np.sin(phase), axis=0) / count


def operator_table(count):
    column = operator_column(count)
    steps = np.arange(count)
    offsets = (steps[None, :] - steps[:, None]) % count
    return column[offsets].astype(np.float32)


def block_weights(count):
    table = operator_table(count)
    width = 128
    w_self = table[:width, :width]
    w_prev = table[:width, width : 2 * width]
    w_next = table[width : 2 * width, :width]
    return jnp.asarray(np.concatenate([w_prev, w_self, w_next], axis=1))


def column_basis(block, tol=1e-12):
    rest = block.copy()
    basis = []
    while len(basis) < block.shape[1]:
        norms = np.sqrt(np.sum(rest * rest, axis=0))
        pick = int(np.argmax(norms))
        if norms[pick] <= tol:
            break
        vec = rest[:, pick].copy()
        for _ in range(2):
            for q in basis:
                vec = vec - np.sum(q * vec) * q
        vec = vec / np.sqrt(np.sum(vec * vec))
        basis.append(vec)
        rest = rest - vec[:, None] * np.sum(vec[:, None] * rest, axis=0)[None, :]
    return basis


def y_operator(rows, groups):
    count = rows * groups
    column = operator_column(count)
    steps = np.arange(count)
    full = column[(steps[:, None] - steps[None, :]) % count]
    own = full[:rows, :rows].astype(np.float32)
    shifts = []
    for e in range(1, groups):
        block = full[:rows, rows * e : rows * (e + 1)]
        basis = column_basis(block)
        if not basis:
            continue
        q = np.stack(basis, axis=1)
        w = np.sum(q[:, :, None] * block[:, None, :], axis=0)
        shifts.append((e, q.astype(np.float32), w.astype(np.float32)))
    return own, shifts


HI = lax.Precision.HIGHEST
WIDTH = 128


def dot(a, b):
    return jnp.dot(a, b, precision=HI, preferred_element_type=jnp.float32)


def plane_fluxes(rho_ref, mom_ref, energy_ref):
    rho = rho_ref[0]
    m_x = mom_ref[0, 0]
    m_y = mom_ref[1, 0]
    m_z = mom_ref[2, 0]
    energy = energy_ref[0]
    vel_x = m_x / rho
    vel_y = m_y / rho
    pressure = 0.4 * (energy - 0.5 * (m_x * m_x + m_y * m_y + m_z * m_z) / rho)
    enthalpy = energy + pressure
    flux_x = (m_x, m_x * vel_x + pressure, m_y * vel_x, m_z * vel_x, enthalpy * vel_x)
    flux_y = (m_y, m_x * vel_y, m_y * vel_y + pressure, m_z * vel_y, enthalpy * vel_y)
    return flux_x, flux_y


def moments_kernel(splits, weights_ref, rho_ref, mom_ref, energy_ref, *out_refs):
    _, flux_y = plane_fluxes(rho_ref, mom_ref, energy_ref)
    weights = weights_ref[...]
    for f in range(5):
        moments = dot(weights, flux_y[f])
        for (lo, hi), out_ref in zip(splits, out_refs):
            out_ref[0, f] = moments[lo:hi]


def tendency_kernel(count, wx_ref, own_ref, spread_ref, rho_ref, mom_ref, energy_ref, *refs):
    recv_refs, out_ref = refs[:-1], refs[-1]
    flux_x, flux_y = plane_fluxes(rho_ref, mom_ref, energy_ref)
    wx = wx_ref[...]
    own = own_ref[...]
    spread = spread_ref[...]
    nb = count // WIDTH
    for f in range(5):
        received = jnp.concatenate([r[0, f] for r in recv_refs], axis=0)
        d_y = dot(own, flux_y[f]) + dot(spread, received)
        fx = flux_x[f]
        rows = fx.shape[0]
        stacked = jnp.concatenate([fx[:, b * WIDTH : (b + 1) * WIDTH] for b in range(nb)], axis=0)
        parts = dot(stacked, wx)
        for b in range(nb):
            bp = (b - 1) % nb
            bn = (b + 1) % nb
            d_x = (
                parts[bp * rows : (bp + 1) * rows, :WIDTH]
                + parts[b * rows : (b + 1) * rows, WIDTH : 2 * WIDTH]
                + parts[bn * rows : (bn + 1) * rows, 2 * WIDTH :]
            )
            out_ref[f, 0, :, b * WIDTH : (b + 1) * WIDTH] = -(d_x + d_y[:, b * WIDTH : (b + 1) * WIDTH])


def full_spec(shape):
    return pl.BlockSpec(shape, lambda z: (0,) * len(shape))


def make_local(groups):
    def local(density, momentum, energy):
        planes, rows, count = density.shape
        own, shifts = y_operator(rows, groups)
        weights = np.concatenate([w for _, _, w in shifts], axis=0)
        spread = np.concatenate([q for _, q, _ in shifts], axis=1)
        splits = []
        lo = 0
        for _, _, w in shifts:
            splits.append((lo, lo + w.shape[0]))
            lo += w.shape[0]
        plane_specs = [
            pl.BlockSpec((1, rows, count), lambda z: (z, 0, 0)),
            pl.BlockSpec((3, 1, rows, count), lambda z: (0, z, 0, 0)),
            pl.BlockSpec((1, rows, count), lambda z: (z, 0, 0)),
        ]
        moment_shapes = [
            jax.ShapeDtypeStruct((planes, 5, hi - lo, count), jnp.float32) for lo, hi in splits
        ]
        moment_specs = [
            pl.BlockSpec((1, 5, hi - lo, count), lambda z: (z, 0, 0, 0)) for lo, hi in splits
        ]
        moments = pl.pallas_call(
            lambda *r: moments_kernel(splits, *r),
            grid=(planes,),
            in_specs=[full_spec(weights.shape)] + plane_specs,
            out_specs=moment_specs,
            out_shape=moment_shapes,
        )(jnp.asarray(weights), density, momentum, energy)
        received = [
            lax.ppermute(part, "row", [(j, (j - e) % groups) for j in range(groups)])
            for (e, _, _), part in zip(shifts, moments)
        ]
        wx = block_weights(count)
        return pl.pallas_call(
            lambda *r: tendency_kernel(count, *r),
            grid=(planes,),
            in_specs=[full_spec(wx.shape), full_spec(own.shape), full_spec(spread.shape)]
            + plane_specs
            + moment_specs,
            out_specs=pl.BlockSpec((5, 1, rows, count), lambda z: (0, z, 0, 0)),
            out_shape=jax.ShapeDtypeStruct((5, planes, rows, count), jnp.float32),
        )(wx, jnp.asarray(own), jnp.asarray(spread), density, momentum, energy, *received)

    return local


def solution(mesh):
    in_specs = (P("col", "row", None), P(None, "col", "row", None), P("col", "row", None))
    out_specs = P(None, "col", "row", None)
    return jax.shard_map(
        make_local(mesh.shape["row"]),
        mesh=mesh,
        in_specs=in_specs,
        out_specs=out_specs,
        check_vma=False,
    )
```

```python
import jax
import jax.numpy as jnp
import numpy as np
from jax import lax
from jax.experimental import pallas as pl
from jax.experimental.pallas import tpu as pltpu
from jax.sharding import PartitionSpec as P


def operator_column(count):
    steps = np.arange(count)
    wave = 2.0 * np.pi * steps / count
    upper = (
        17.0 / 12.0 * np.sin(wave)
        + 101.0 / 300.0 * np.sin(2.0 * wave)
        + 1.0 / 300.0 * np.sin(3.0 * wave)
    )
    lower = 1.0 + np.cos(wave) + 0.1 * np.cos(2.0 * wave)
    ratio = upper / lower
    phase = 2.0 * np.pi * (steps[:, None] * steps[None, :] % count) / count
    return -np.sum(ratio[:, None] * np.sin(phase), axis=0) / count


def operator_table(count):
    column = operator_column(count)
    steps = np.arange(count)
    offsets = (steps[None, :] - steps[:, None]) % count
    return column[offsets].astype(np.float32)


def block_weights(count):
    table = operator_table(count)
    width = 128
    w_self = table[:width, :width]
    w_prev = table[:width, width : 2 * width]
    w_next = table[width : 2 * width, :width]
    return jnp.asarray(np.concatenate([w_prev, w_self, w_next], axis=1))


def column_basis(block, tol=1e-12):
    rest = block.copy()
    basis = []
    while len(basis) < block.shape[1]:
        norms = np.sqrt(np.sum(rest * rest, axis=0))
        pick = int(np.argmax(norms))
        if norms[pick] <= tol:
            break
        vec = rest[:, pick].copy()
        for _ in range(2):
            for q in basis:
                vec = vec - np.sum(q * vec) * q
        vec = vec / np.sqrt(np.sum(vec * vec))
        basis.append(vec)
        rest = rest - vec[:, None] * np.sum(vec[:, None] * rest, axis=0)[None, :]
    return basis


def y_operator(rows, groups):
    count = rows * groups
    column = operator_column(count)
    steps = np.arange(count)
    full = column[(steps[:, None] - steps[None, :]) % count]
    own = full[:rows, :rows].astype(np.float32)
    shifts = []
    for e in range(1, groups):
        block = full[:rows, rows * e : rows * (e + 1)]
        basis = column_basis(block)
        if not basis:
            continue
        q = np.stack(basis, axis=1)
        w = np.sum(q[:, :, None] * block[:, None, :], axis=0)
        shifts.append((e, q.astype(np.float32), w.astype(np.float32)))
    return own, shifts


HI = lax.Precision.HIGHEST
WIDTH = 128


def dot(a, b):
    return jnp.dot(a, b, precision=HI, preferred_element_type=jnp.float32)


def plane_fluxes(rho_ref, mom_ref, energy_ref):
    rho = rho_ref[0]
    m_x = mom_ref[0, 0]
    m_y = mom_ref[1, 0]
    m_z = mom_ref[2, 0]
    energy = energy_ref[0]
    vel_x = m_x / rho
    vel_y = m_y / rho
    pressure = 0.4 * (energy - 0.5 * (m_x * m_x + m_y * m_y + m_z * m_z) / rho)
    enthalpy = energy + pressure
    flux_x = (m_x, m_x * vel_x + pressure, m_y * vel_x, m_z * vel_x, enthalpy * vel_x)
    flux_y = (m_y, m_x * vel_y, m_y * vel_y + pressure, m_z * vel_y, enthalpy * vel_y)
    return flux_x, flux_y


def moments_kernel(splits, weights_ref, rho_ref, mom_ref, energy_ref, *out_refs):
    _, flux_y = plane_fluxes(rho_ref, mom_ref, energy_ref)
    weights = weights_ref[...]
    for f in range(5):
        moments = dot(weights, flux_y[f])
        for (lo, hi), out_ref in zip(splits, out_refs):
            out_ref[0, f] = moments[lo:hi]


def local_kernel(count, wx_ref, own_ref, rho_ref, mom_ref, energy_ref, out_ref):
    flux_x, flux_y = plane_fluxes(rho_ref, mom_ref, energy_ref)
    wx = wx_ref[...]
    own = own_ref[...]
    nb = count // WIDTH
    for f in range(5):
        d_y = dot(own, flux_y[f])
        fx = flux_x[f]
        rows = fx.shape[0]
        stacked = jnp.concatenate([fx[:, b * WIDTH : (b + 1) * WIDTH] for b in range(nb)], axis=0)
        parts = dot(stacked, wx)
        for b in range(nb):
            bp = (b - 1) % nb
            bn = (b + 1) % nb
            d_x = (
                parts[bp * rows : (bp + 1) * rows, :WIDTH]
                + parts[b * rows : (b + 1) * rows, WIDTH : 2 * WIDTH]
                + parts[bn * rows : (bn + 1) * rows, 2 * WIDTH :]
            )
            out_ref[f, 0, :, b * WIDTH : (b + 1) * WIDTH] = -(d_x + d_y[:, b * WIDTH : (b + 1) * WIDTH])


def correct_kernel(spread_ref, partial_ref, *refs):
    recv_refs, out_ref = refs[:-1], refs[-1]
    spread = spread_ref[...]
    for f in range(5):
        received = jnp.concatenate([r[0, f] for r in recv_refs], axis=0)
        out_ref[f, 0] = partial_ref[f, 0] - dot(spread, received)


def full_spec(shape):
    return pl.BlockSpec(shape, lambda z: (0,) * len(shape))


def make_local(groups):
    def local(density, momentum, energy):
        planes, rows, count = density.shape
        own, shifts = y_operator(rows, groups)
        weights = np.concatenate([w for _, _, w in shifts], axis=0)
        spread = np.concatenate([q for _, q, _ in shifts], axis=1)
        splits = []
        lo = 0
        for _, _, w in shifts:
            splits.append((lo, lo + w.shape[0]))
            lo += w.shape[0]
        plane_specs = [
            pl.BlockSpec((1, rows, count), lambda z: (z, 0, 0)),
            pl.BlockSpec((3, 1, rows, count), lambda z: (0, z, 0, 0)),
            pl.BlockSpec((1, rows, count), lambda z: (z, 0, 0)),
        ]
        moment_shapes = [
            jax.ShapeDtypeStruct((planes, 5, hi - lo, count), jnp.float32) for lo, hi in splits
        ]
        moment_specs = [
            pl.BlockSpec((1, 5, hi - lo, count), lambda z: (z, 0, 0, 0)) for lo, hi in splits
        ]
        moments = pl.pallas_call(
            lambda *r: moments_kernel(splits, *r),
            grid=(planes,),
            in_specs=[full_spec(weights.shape)] + plane_specs,
            out_specs=moment_specs,
            out_shape=moment_shapes,
        )(jnp.asarray(weights), density, momentum, energy)
        received = [
            lax.ppermute(part, "row", [(j, (j - e) % groups) for j in range(groups)])
            for (e, _, _), part in zip(shifts, moments)
        ]
        wx = block_weights(count)
        out_spec = pl.BlockSpec((5, 1, rows, count), lambda z: (0, z, 0, 0))
        out_shape = jax.ShapeDtypeStruct((5, planes, rows, count), jnp.float32)
        partial = pl.pallas_call(
            lambda *r: local_kernel(count, *r),
            grid=(planes,),
            in_specs=[full_spec(wx.shape), full_spec(own.shape)] + plane_specs,
            out_specs=out_spec,
            out_shape=out_shape,
        )(wx, jnp.asarray(own), density, momentum, energy)
        return pl.pallas_call(
            correct_kernel,
            grid=(planes,),
            in_specs=[full_spec(spread.shape), out_spec] + moment_specs,
            out_specs=out_spec,
            out_shape=out_shape,
            input_output_aliases={1: 0},
        )(jnp.asarray(spread), partial, *received)

    return local


def solution(mesh):
    in_specs = (P("col", "row", None), P(None, "col", "row", None), P("col", "row", None))
    out_specs = P(None, "col", "row", None)
    return jax.shard_map(
        make_local(mesh.shape["row"]),
        mesh=mesh,
        in_specs=in_specs,
        out_specs=out_specs,
        check_vma=False,
    )
```

```python
import jax
import jax.numpy as jnp
import numpy as np
from jax import lax
from jax.experimental import pallas as pl
from jax.experimental.pallas import tpu as pltpu
from jax.sharding import PartitionSpec as P


def operator_column(count):
    steps = np.arange(count)
    wave = 2.0 * np.pi * steps / count
    upper = (
        17.0 / 12.0 * np.sin(wave)
        + 101.0 / 300.0 * np.sin(2.0 * wave)
        + 1.0 / 300.0 * np.sin(3.0 * wave)
    )
    lower = 1.0 + np.cos(wave) + 0.1 * np.cos(2.0 * wave)
    ratio = upper / lower
    phase = 2.0 * np.pi * (steps[:, None] * steps[None, :] % count) / count
    return -np.sum(ratio[:, None] * np.sin(phase), axis=0) / count


def operator_table(count):
    column = operator_column(count)
    steps = np.arange(count)
    offsets = (steps[None, :] - steps[:, None]) % count
    return column[offsets].astype(np.float32)


def block_weights(count):
    table = operator_table(count)
    width = 128
    w_self = table[:width, :width]
    w_prev = table[:width, width : 2 * width]
    w_next = table[width : 2 * width, :width]
    return jnp.asarray(np.concatenate([w_prev, w_self, w_next], axis=1))


def column_basis(block, tol=1e-12):
    rest = block.copy()
    basis = []
    while len(basis) < block.shape[1]:
        norms = np.sqrt(np.sum(rest * rest, axis=0))
        pick = int(np.argmax(norms))
        if norms[pick] <= tol:
            break
        vec = rest[:, pick].copy()
        for _ in range(2):
            for q in basis:
                vec = vec - np.sum(q * vec) * q
        vec = vec / np.sqrt(np.sum(vec * vec))
        basis.append(vec)
        rest = rest - vec[:, None] * np.sum(vec[:, None] * rest, axis=0)[None, :]
    return basis


def y_operator(rows, groups):
    count = rows * groups
    column = operator_column(count)
    steps = np.arange(count)
    full = column[(steps[:, None] - steps[None, :]) % count]
    own = full[:rows, :rows].astype(np.float32)
    shifts = []
    for e in range(1, groups):
        block = full[:rows, rows * e : rows * (e + 1)]
        basis = column_basis(block)
        if not basis:
            continue
        q = np.stack(basis, axis=1)
        w = np.sum(q[:, :, None] * block[:, None, :], axis=0)
        shifts.append((e, q.astype(np.float32), w.astype(np.float32)))
    return own, shifts


HI = lax.Precision.HIGHEST
WIDTH = 128


def dot(a, b):
    return jnp.dot(a, b, precision=HI, preferred_element_type=jnp.float32)


def plane_fluxes(rho_ref, mom_ref, energy_ref):
    rho = rho_ref[0]
    m_x = mom_ref[0, 0]
    m_y = mom_ref[1, 0]
    m_z = mom_ref[2, 0]
    energy = energy_ref[0]
    vel_x = m_x / rho
    vel_y = m_y / rho
    pressure = 0.4 * (energy - 0.5 * (m_x * m_x + m_y * m_y + m_z * m_z) / rho)
    enthalpy = energy + pressure
    flux_x = (m_x, m_x * vel_x + pressure, m_y * vel_x, m_z * vel_x, enthalpy * vel_x)
    flux_y = (m_y, m_x * vel_y, m_y * vel_y + pressure, m_z * vel_y, enthalpy * vel_y)
    return flux_x, flux_y


def moments_kernel(splits, weights_ref, rho_ref, mom_ref, energy_ref, *out_refs):
    _, flux_y = plane_fluxes(rho_ref, mom_ref, energy_ref)
    weights = weights_ref[...]
    for f in range(5):
        moments = dot(weights, flux_y[f])
        for (lo, hi), out_ref in zip(splits, out_refs):
            out_ref[0, f] = moments[lo:hi]


def local_kernel(count, wx_ref, own_ref, rho_ref, mom_ref, energy_ref, out_ref):
    flux_x, flux_y = plane_fluxes(rho_ref, mom_ref, energy_ref)
    wx = wx_ref[...]
    own = own_ref[...]
    nb = count // WIDTH
    for f in range(5):
        d_y = dot(own, flux_y[f])
        fx = flux_x[f]
        rows = fx.shape[0]
        stacked = jnp.concatenate([fx[:, b * WIDTH : (b + 1) * WIDTH] for b in range(nb)], axis=0)
        parts = dot(stacked, wx)
        for b in range(nb):
            bp = (b - 1) % nb
            bn = (b + 1) % nb
            d_x = (
                parts[bp * rows : (bp + 1) * rows, :WIDTH]
                + parts[b * rows : (b + 1) * rows, WIDTH : 2 * WIDTH]
                + parts[bn * rows : (bn + 1) * rows, 2 * WIDTH :]
            )
            out_ref[f, 0, :, b * WIDTH : (b + 1) * WIDTH] = -(d_x + d_y[:, b * WIDTH : (b + 1) * WIDTH])


def correct_kernel(nrecv, partial_ref, *refs):
    spread_refs, recv_refs, out_ref = refs[:nrecv], refs[nrecv:-1], refs[-1]
    acc = partial_ref[0, 0]
    for spread_ref, recv_ref in zip(spread_refs, recv_refs):
        spread = spread_ref[...]
        received = recv_ref[0, 0]
        for r in range(received.shape[0]):
            acc = acc - spread[:, r : r + 1] * received[r : r + 1, :]
    out_ref[0, 0] = acc


def full_spec(shape):
    return pl.BlockSpec(shape, lambda z: (0,) * len(shape))


def make_local(groups):
    def local(density, momentum, energy):
        planes, rows, count = density.shape
        own, shifts = y_operator(rows, groups)
        weights = np.concatenate([w for _, _, w in shifts], axis=0)
        splits = []
        lo = 0
        for _, _, w in shifts:
            splits.append((lo, lo + w.shape[0]))
            lo += w.shape[0]
        plane_specs = [
            pl.BlockSpec((1, rows, count), lambda z: (z, 0, 0)),
            pl.BlockSpec((3, 1, rows, count), lambda z: (0, z, 0, 0)),
            pl.BlockSpec((1, rows, count), lambda z: (z, 0, 0)),
        ]
        chunk = 512 if count % 512 == 0 else count
        chunk_specs = [
            pl.BlockSpec((1, rows, chunk), lambda z, c: (z, 0, c)),
            pl.BlockSpec((3, 1, rows, chunk), lambda z, c: (0, z, 0, c)),
            pl.BlockSpec((1, rows, chunk), lambda z, c: (z, 0, c)),
        ]
        moment_shapes = [
            jax.ShapeDtypeStruct((planes, 5, hi - lo, count), jnp.float32) for lo, hi in splits
        ]
        moments = pl.pallas_call(
            lambda *r: moments_kernel(splits, *r),
            grid=(planes, count // chunk),
            in_specs=[pl.BlockSpec(weights.shape, lambda z, c: (0, 0))] + chunk_specs,
            out_specs=[
                pl.BlockSpec((1, 5, hi - lo, chunk), lambda z, c: (z, 0, 0, c)) for lo, hi in splits
            ],
            out_shape=moment_shapes,
        )(jnp.asarray(weights), density, momentum, energy)
        received = [
            lax.ppermute(part, "row", [(j, (j - e) % groups) for j in range(groups)])
            for (e, _, _), part in zip(shifts, moments)
        ]
        wx = block_weights(count)
        out_spec = pl.BlockSpec((5, 1, rows, count), lambda z: (0, z, 0, 0))
        out_shape = jax.ShapeDtypeStruct((5, planes, rows, count), jnp.float32)
        partial = pl.pallas_call(
            lambda *r: local_kernel(count, *r),
            grid=(planes,),
            in_specs=[full_spec(wx.shape), full_spec(own.shape)] + plane_specs,
            out_specs=out_spec,
            out_shape=out_shape,
        )(wx, jnp.asarray(own), density, momentum, energy)
        field_spec = pl.BlockSpec((1, 1, rows, count), lambda z, f: (f, z, 0, 0))
        spreads = [jnp.asarray(q) for _, q, _ in shifts]
        return pl.pallas_call(
            lambda *r: correct_kernel(len(shifts), *r),
            grid=(planes, 5),
            in_specs=[field_spec]
            + [pl.BlockSpec(q.shape, lambda z, f: (0, 0)) for q in spreads]
            + [
                pl.BlockSpec((1, 1, hi - lo, count), lambda z, f: (z, f, 0, 0))
                for lo, hi in splits
            ],
            out_specs=field_spec,
            out_shape=out_shape,
            input_output_aliases={0: 0},
        )(partial, *spreads, *received)

    return local


def solution(mesh):
    in_specs = (P("col", "row", None), P(None, "col", "row", None), P("col", "row", None))
    out_specs = P(None, "col", "row", None)
    return jax.shard_map(
        make_local(mesh.shape["row"]),
        mesh=mesh,
        in_specs=in_specs,
        out_specs=out_specs,
        check_vma=False,
    )
```

```python
import jax
import jax.numpy as jnp
import numpy as np
from jax import lax
from jax.experimental import pallas as pl
from jax.experimental.pallas import tpu as pltpu
from jax.sharding import PartitionSpec as P


def operator_column(count):
    steps = np.arange(count)
    wave = 2.0 * np.pi * steps / count
    upper = (
        17.0 / 12.0 * np.sin(wave)
        + 101.0 / 300.0 * np.sin(2.0 * wave)
        + 1.0 / 300.0 * np.sin(3.0 * wave)
    )
    lower = 1.0 + np.cos(wave) + 0.1 * np.cos(2.0 * wave)
    ratio = upper / lower
    phase = 2.0 * np.pi * (steps[:, None] * steps[None, :] % count) / count
    return -np.sum(ratio[:, None] * np.sin(phase), axis=0) / count


def operator_table(count):
    column = operator_column(count)
    steps = np.arange(count)
    offsets = (steps[None, :] - steps[:, None]) % count
    return column[offsets].astype(np.float32)


def block_weights(count):
    table = operator_table(count)
    width = 128
    w_self = table[:width, :width]
    w_prev = table[:width, width : 2 * width]
    w_next = table[width : 2 * width, :width]
    return jnp.asarray(np.concatenate([w_prev, w_self, w_next], axis=1))


def column_basis(block, tol=1e-12):
    rest = block.copy()
    basis = []
    while len(basis) < block.shape[1]:
        norms = np.sqrt(np.sum(rest * rest, axis=0))
        pick = int(np.argmax(norms))
        if norms[pick] <= tol:
            break
        vec = rest[:, pick].copy()
        for _ in range(2):
            for q in basis:
                vec = vec - np.sum(q * vec) * q
        vec = vec / np.sqrt(np.sum(vec * vec))
        basis.append(vec)
        rest = rest - vec[:, None] * np.sum(vec[:, None] * rest, axis=0)[None, :]
    return basis


def y_operator(rows, groups):
    count = rows * groups
    column = operator_column(count)
    steps = np.arange(count)
    full = column[(steps[:, None] - steps[None, :]) % count]
    own = full[:rows, :rows].astype(np.float32)
    shifts = []
    for e in range(1, groups):
        block = full[:rows, rows * e : rows * (e + 1)]
        basis = column_basis(block)
        if not basis:
            continue
        q = np.stack(basis, axis=1)
        w = np.sum(q[:, :, None] * block[:, None, :], axis=0)
        shifts.append((e, q.astype(np.float32), w.astype(np.float32)))
    return own, shifts


HI = lax.Precision.HIGHEST
WIDTH = 128


def dot(a, b):
    return jnp.dot(a, b, precision=HI, preferred_element_type=jnp.float32)


def plane_fluxes(rho_ref, mom_ref, energy_ref):
    rho = rho_ref[0]
    m_x = mom_ref[0, 0]
    m_y = mom_ref[1, 0]
    m_z = mom_ref[2, 0]
    energy = energy_ref[0]
    vel_x = m_x / rho
    vel_y = m_y / rho
    pressure = 0.4 * (energy - 0.5 * (m_x * m_x + m_y * m_y + m_z * m_z) / rho)
    enthalpy = energy + pressure
    flux_x = (m_x, m_x * vel_x + pressure, m_y * vel_x, m_z * vel_x, enthalpy * vel_x)
    flux_y = (m_y, m_x * vel_y, m_y * vel_y + pressure, m_z * vel_y, enthalpy * vel_y)
    return flux_x, flux_y


def moments_kernel(splits, weights_ref, rho_ref, mom_ref, energy_ref, *out_refs):
    _, flux_y = plane_fluxes(rho_ref, mom_ref, energy_ref)
    weights = weights_ref[...]
    for f in range(5):
        moments = dot(weights, flux_y[f])
        for (lo, hi), out_ref in zip(splits, out_refs):
            out_ref[0, f] = moments[lo:hi]


def local_kernel(count, wx_ref, own_ref, rho_ref, mom_ref, energy_ref, out_ref):
    flux_x, flux_y = plane_fluxes(rho_ref, mom_ref, energy_ref)
    wx = wx_ref[...]
    own = own_ref[...]
    nb = count // WIDTH
    for f in range(5):
        d_y = dot(own, flux_y[f])
        fx = flux_x[f]
        rows = fx.shape[0]
        stacked = jnp.concatenate([fx[:, b * WIDTH : (b + 1) * WIDTH] for b in range(nb)], axis=0)
        parts = dot(stacked, wx)
        for b in range(nb):
            bp = (b - 1) % nb
            bn = (b + 1) % nb
            d_x = (
                parts[bp * rows : (bp + 1) * rows, :WIDTH]
                + parts[b * rows : (b + 1) * rows, WIDTH : 2 * WIDTH]
                + parts[bn * rows : (bn + 1) * rows, 2 * WIDTH :]
            )
            out_ref[f, 0, :, b * WIDTH : (b + 1) * WIDTH] = -(d_x + d_y[:, b * WIDTH : (b + 1) * WIDTH])


def full_spec(shape):
    return pl.BlockSpec(shape, lambda z: (0,) * len(shape))


def make_local(groups):
    def local(density, momentum, energy):
        planes, rows, count = density.shape
        own, shifts = y_operator(rows, groups)
        weights = np.concatenate([w for _, _, w in shifts], axis=0)
        spread = np.concatenate([q for _, q, _ in shifts], axis=1)
        splits = []
        lo = 0
        for _, _, w in shifts:
            splits.append((lo, lo + w.shape[0]))
            lo += w.shape[0]
        plane_specs = [
            pl.BlockSpec((1, rows, count), lambda z: (z, 0, 0)),
            pl.BlockSpec((3, 1, rows, count), lambda z: (0, z, 0, 0)),
            pl.BlockSpec((1, rows, count), lambda z: (z, 0, 0)),
        ]
        moment_shapes = [
            jax.ShapeDtypeStruct((planes, 5, hi - lo, count), jnp.float32) for lo, hi in splits
        ]
        moment_specs = [
            pl.BlockSpec((1, 5, hi - lo, count), lambda z: (z, 0, 0, 0)) for lo, hi in splits
        ]
        moments = pl.pallas_call(
            lambda *r: moments_kernel(splits, *r),
            grid=(planes,),
            in_specs=[full_spec(weights.shape)] + plane_specs,
            out_specs=moment_specs,
            out_shape=moment_shapes,
        )(jnp.asarray(weights), density, momentum, energy)
        received = [
            lax.ppermute(part, "row", [(j, (j - e) % groups) for j in range(groups)])
            for (e, _, _), part in zip(shifts, moments)
        ]
        wx = block_weights(count)
        out_spec = pl.BlockSpec((5, 1, rows, count), lambda z: (0, z, 0, 0))
        out_shape = jax.ShapeDtypeStruct((5, planes, rows, count), jnp.float32)
        partial = pl.pallas_call(
            lambda *r: local_kernel(count, *r),
            grid=(planes,),
            in_specs=[full_spec(wx.shape), full_spec(own.shape)] + plane_specs,
            out_specs=out_spec,
            out_shape=out_shape,
        )(wx, jnp.asarray(own), density, momentum, energy)
        received = jnp.concatenate(received, axis=2)
        return partial - jnp.einsum(
            "pr,zfrx->fzpx", jnp.asarray(spread), received, precision=HI
        )

    return local


def solution(mesh):
    in_specs = (P("col", "row", None), P(None, "col", "row", None), P("col", "row", None))
    out_specs = P(None, "col", "row", None)
    return jax.shard_map(
        make_local(mesh.shape["row"]),
        mesh=mesh,
        in_specs=in_specs,
        out_specs=out_specs,
        check_vma=False,
    )
```

```python
import jax
import jax.numpy as jnp
import numpy as np
from jax import lax
from jax.experimental import pallas as pl
from jax.experimental.pallas import tpu as pltpu
from jax.sharding import PartitionSpec as P


def operator_column(count):
    steps = np.arange(count)
    wave = 2.0 * np.pi * steps / count
    upper = (
        17.0 / 12.0 * np.sin(wave)
        + 101.0 / 300.0 * np.sin(2.0 * wave)
        + 1.0 / 300.0 * np.sin(3.0 * wave)
    )
    lower = 1.0 + np.cos(wave) + 0.1 * np.cos(2.0 * wave)
    ratio = upper / lower
    phase = 2.0 * np.pi * (steps[:, None] * steps[None, :] % count) / count
    return -np.sum(ratio[:, None] * np.sin(phase), axis=0) / count


def operator_table(count):
    column = operator_column(count)
    steps = np.arange(count)
    offsets = (steps[None, :] - steps[:, None]) % count
    return column[offsets].astype(np.float32)


def block_weights(count):
    table = operator_table(count)
    width = 128
    w_self = table[:width, :width]
    w_prev = table[:width, width : 2 * width]
    w_next = table[width : 2 * width, :width]
    return jnp.asarray(np.concatenate([w_prev, w_self, w_next], axis=1))


def column_basis(block, tol=1e-12):
    rest = block.copy()
    basis = []
    while len(basis) < block.shape[1]:
        norms = np.sqrt(np.sum(rest * rest, axis=0))
        pick = int(np.argmax(norms))
        if norms[pick] <= tol:
            break
        vec = rest[:, pick].copy()
        for _ in range(2):
            for q in basis:
                vec = vec - np.sum(q * vec) * q
        vec = vec / np.sqrt(np.sum(vec * vec))
        basis.append(vec)
        rest = rest - vec[:, None] * np.sum(vec[:, None] * rest, axis=0)[None, :]
    return basis


def y_operator(rows, groups):
    count = rows * groups
    column = operator_column(count)
    steps = np.arange(count)
    full = column[(steps[:, None] - steps[None, :]) % count]
    own = full[:rows, :rows].astype(np.float32)
    shifts = []
    for e in range(1, groups):
        block = full[:rows, rows * e : rows * (e + 1)]
        basis = column_basis(block)
        if not basis:
            continue
        q = np.stack(basis, axis=1)
        w = np.sum(q[:, :, None] * block[:, None, :], axis=0)
        shifts.append((e, q.astype(np.float32), w.astype(np.float32)))
    return own, shifts


HI = lax.Precision.HIGHEST
WIDTH = 128


def dot(a, b):
    return jnp.dot(a, b, precision=HI, preferred_element_type=jnp.float32)


def plane_fluxes(rho_ref, mom_ref, energy_ref):
    rho = rho_ref[0]
    m_x = mom_ref[0, 0]
    m_y = mom_ref[1, 0]
    m_z = mom_ref[2, 0]
    energy = energy_ref[0]
    vel_x = m_x / rho
    vel_y = m_y / rho
    pressure = 0.4 * (energy - 0.5 * (m_x * m_x + m_y * m_y + m_z * m_z) / rho)
    enthalpy = energy + pressure
    flux_x = (m_x, m_x * vel_x + pressure, m_y * vel_x, m_z * vel_x, enthalpy * vel_x)
    flux_y = (m_y, m_x * vel_y, m_y * vel_y + pressure, m_z * vel_y, enthalpy * vel_y)
    return flux_x, flux_y


def moments_kernel(splits, weights_ref, rho_ref, mom_ref, energy_ref, *out_refs):
    _, flux_y = plane_fluxes(rho_ref, mom_ref, energy_ref)
    weights = weights_ref[...]
    for f in range(5):
        moments = dot(weights, flux_y[f])
        for (lo, hi), out_ref in zip(splits, out_refs):
            out_ref[0, f] = moments[lo:hi]


def local_kernel(count, wx_ref, own_ref, rho_ref, mom_ref, energy_ref, out_ref):
    flux_x, flux_y = plane_fluxes(rho_ref, mom_ref, energy_ref)
    wx = wx_ref[...]
    own = own_ref[...]
    nb = count // WIDTH
    for f in range(5):
        d_y = dot(own, flux_y[f])
        fx = flux_x[f]
        rows = fx.shape[0]
        stacked = jnp.concatenate([fx[:, b * WIDTH : (b + 1) * WIDTH] for b in range(nb)], axis=0)
        parts = dot(stacked, wx)
        for b in range(nb):
            bp = (b - 1) % nb
            bn = (b + 1) % nb
            d_x = (
                parts[bp * rows : (bp + 1) * rows, :WIDTH]
                + parts[b * rows : (b + 1) * rows, WIDTH : 2 * WIDTH]
                + parts[bn * rows : (bn + 1) * rows, 2 * WIDTH :]
            )
            out_ref[f, 0, :, b * WIDTH : (b + 1) * WIDTH] = -(d_x + d_y[:, b * WIDTH : (b + 1) * WIDTH])


def exchange_plan(groups, shift_list):
    if groups % 4 or sorted(shift_list) != sorted({1, 2, groups - 2, groups - 1}) or groups < 8:
        return None
    plans = []
    for step, phase in ((1, 0), (1, 1), (2, 0), (2, 1)):
        perm = []
        sends_first = np.zeros(groups, bool)
        takes_first = np.zeros(groups, bool)
        for r in range(groups):
            if (r // step) % 2 == phase:
                up = (r + step) % groups
                perm += [(r, up), (up, r)]
                sends_first[up] = True
                takes_first[r] = True
        plans.append((perm, sends_first, takes_first, step, groups - step))
    return plans


def full_spec(shape):
    return pl.BlockSpec(shape, lambda z: (0,) * len(shape))


def make_local(groups):
    def local(density, momentum, energy):
        planes, rows, count = density.shape
        own, shifts = y_operator(rows, groups)
        weights = np.concatenate([w for _, _, w in shifts], axis=0)
        splits = []
        lo = 0
        for _, _, w in shifts:
            splits.append((lo, lo + w.shape[0]))
            lo += w.shape[0]
        plane_specs = [
            pl.BlockSpec((1, rows, count), lambda z: (z, 0, 0)),
            pl.BlockSpec((3, 1, rows, count), lambda z: (0, z, 0, 0)),
            pl.BlockSpec((1, rows, count), lambda z: (z, 0, 0)),
        ]
        moment_shapes = [
            jax.ShapeDtypeStruct((planes, 5, hi - lo, count), jnp.float32) for lo, hi in splits
        ]
        moment_specs = [
            pl.BlockSpec((1, 5, hi - lo, count), lambda z: (z, 0, 0, 0)) for lo, hi in splits
        ]
        moments = pl.pallas_call(
            lambda *r: moments_kernel(splits, *r),
            grid=(planes,),
            in_specs=[full_spec(weights.shape)] + plane_specs,
            out_specs=moment_specs,
            out_shape=moment_shapes,
        )(jnp.asarray(weights), density, momentum, energy)
        by_shift = {e: (q, part) for (e, q, _), part in zip(shifts, moments)}
        pairs = exchange_plan(groups, [e for e, _, _ in shifts])
        if pairs is None:
            received = [
                lax.ppermute(part, "row", [(j, (j - e) % groups) for j in range(groups)])
                for (e, _, _), part in zip(shifts, moments)
            ]
            spread = jnp.asarray(np.concatenate([q for _, q, _ in shifts], axis=1))
        else:
            index = lax.axis_index("row")
            received = []
            spreads = []
            for perm, sends_first, takes_first, first, second in pairs:
                send = jnp.asarray(sends_first)[index]
                take = jnp.asarray(takes_first)[index]
                message = jnp.where(send, by_shift[first][1], by_shift[second][1])
                received.append(lax.ppermute(message, "row", perm))
                spreads.append(
                    jnp.where(take, jnp.asarray(by_shift[first][0]), jnp.asarray(by_shift[second][0]))
                )
            spread = jnp.concatenate(spreads, axis=1)
        wx = block_weights(count)
        out_spec = pl.BlockSpec((5, 1, rows, count), lambda z: (0, z, 0, 0))
        out_shape = jax.ShapeDtypeStruct((5, planes, rows, count), jnp.float32)
        partial = pl.pallas_call(
            lambda *r: local_kernel(count, *r),
            grid=(planes,),
            in_specs=[full_spec(wx.shape), full_spec(own.shape)] + plane_specs,
            out_specs=out_spec,
            out_shape=out_shape,
        )(wx, jnp.asarray(own), density, momentum, energy)
        received = jnp.concatenate(received, axis=2)
        return partial - jnp.einsum(
            "pr,zfrx->fzpx", spread, received, precision=HI
        )

    return local


def solution(mesh):
    in_specs = (P("col", "row", None), P(None, "col", "row", None), P("col", "row", None))
    out_specs = P(None, "col", "row", None)
    return jax.shard_map(
        make_local(mesh.shape["row"]),
        mesh=mesh,
        in_specs=in_specs,
        out_specs=out_specs,
        check_vma=False,
    )
```

```python
import jax
import jax.numpy as jnp
import numpy as np
from jax import lax
from jax.experimental import pallas as pl
from jax.experimental.pallas import tpu as pltpu
from jax.sharding import PartitionSpec as P


def operator_column(count):
    steps = np.arange(count)
    wave = 2.0 * np.pi * steps / count
    upper = (
        17.0 / 12.0 * np.sin(wave)
        + 101.0 / 300.0 * np.sin(2.0 * wave)
        + 1.0 / 300.0 * np.sin(3.0 * wave)
    )
    lower = 1.0 + np.cos(wave) + 0.1 * np.cos(2.0 * wave)
    ratio = upper / lower
    phase = 2.0 * np.pi * (steps[:, None] * steps[None, :] % count) / count
    return -np.sum(ratio[:, None] * np.sin(phase), axis=0) / count


def operator_table(count):
    column = operator_column(count)
    steps = np.arange(count)
    offsets = (steps[None, :] - steps[:, None]) % count
    return column[offsets].astype(np.float32)


def block_weights(count):
    table = operator_table(count)
    width = 128
    w_self = table[:width, :width]
    w_prev = table[:width, width : 2 * width]
    w_next = table[width : 2 * width, :width]
    return jnp.asarray(np.concatenate([w_prev, w_self, w_next], axis=1))


def column_basis(block, tol=1e-12):
    rest = block.copy()
    basis = []
    while len(basis) < block.shape[1]:
        norms = np.sqrt(np.sum(rest * rest, axis=0))
        pick = int(np.argmax(norms))
        if norms[pick] <= tol:
            break
        vec = rest[:, pick].copy()
        for _ in range(2):
            for q in basis:
                vec = vec - np.sum(q * vec) * q
        vec = vec / np.sqrt(np.sum(vec * vec))
        basis.append(vec)
        rest = rest - vec[:, None] * np.sum(vec[:, None] * rest, axis=0)[None, :]
    return basis


def y_operator(rows, groups):
    count = rows * groups
    column = operator_column(count)
    steps = np.arange(count)
    full = column[(steps[:, None] - steps[None, :]) % count]
    own = full[:rows, :rows].astype(np.float32)
    shifts = []
    for e in range(1, groups):
        block = full[:rows, rows * e : rows * (e + 1)]
        basis = column_basis(block)
        if not basis:
            continue
        q = np.stack(basis, axis=1)
        w = np.sum(q[:, :, None] * block[:, None, :], axis=0)
        shifts.append((e, q.astype(np.float32), w.astype(np.float32)))
    return own, shifts


HI = lax.Precision.HIGHEST
WIDTH = 128


def dot(a, b):
    return jnp.dot(a, b, precision=HI, preferred_element_type=jnp.float32)


def plane_fluxes(rho_ref, mom_ref, energy_ref):
    rho = rho_ref[0]
    m_x = mom_ref[0, 0]
    m_y = mom_ref[1, 0]
    m_z = mom_ref[2, 0]
    energy = energy_ref[0]
    vel_x = m_x / rho
    vel_y = m_y / rho
    pressure = 0.4 * (energy - 0.5 * (m_x * m_x + m_y * m_y + m_z * m_z) / rho)
    enthalpy = energy + pressure
    flux_x = (m_x, m_x * vel_x + pressure, m_y * vel_x, m_z * vel_x, enthalpy * vel_x)
    flux_y = (m_y, m_x * vel_y, m_y * vel_y + pressure, m_z * vel_y, enthalpy * vel_y)
    return flux_x, flux_y


def moments_kernel(splits, choices, index_ref, weights_ref, rho_ref, mom_ref, energy_ref, *out_refs):
    _, flux_y = plane_fluxes(rho_ref, mom_ref, energy_ref)
    weights = weights_ref[...]
    index = index_ref[0]
    for f in range(5):
        moments = dot(weights, flux_y[f])
        for (step, phase, first, second), out_ref in zip(choices, out_refs):
            pick = (index // step) % 2 != phase
            lo, hi = splits[first]
            lo2, hi2 = splits[second]
            out_ref[0, f] = jnp.where(pick, moments[lo:hi], moments[lo2:hi2])


def local_kernel(count, wx_ref, own_ref, rho_ref, mom_ref, energy_ref, out_ref):
    flux_x, flux_y = plane_fluxes(rho_ref, mom_ref, energy_ref)
    wx = wx_ref[...]
    own = own_ref[...]
    nb = count // WIDTH
    for f in range(5):
        d_y = dot(own, flux_y[f])
        fx = flux_x[f]
        rows = fx.shape[0]
        stacked = jnp.concatenate([fx[:, b * WIDTH : (b + 1) * WIDTH] for b in range(nb)], axis=0)
        parts = dot(stacked, wx)
        for b in range(nb):
            bp = (b - 1) % nb
            bn = (b + 1) % nb
            d_x = (
                parts[bp * rows : (bp + 1) * rows, :WIDTH]
                + parts[b * rows : (b + 1) * rows, WIDTH : 2 * WIDTH]
                + parts[bn * rows : (bn + 1) * rows, 2 * WIDTH :]
            )
            out_ref[f, 0, :, b * WIDTH : (b + 1) * WIDTH] = -(d_x + d_y[:, b * WIDTH : (b + 1) * WIDTH])


def exchange_plan(groups, shift_list):
    assert groups % 4 == 0 and groups >= 8
    assert sorted(shift_list) == sorted({1, 2, groups - 2, groups - 1})
    plans = []
    for step, phase in ((1, 0), (1, 1), (2, 0), (2, 1)):
        perm = []
        for r in range(groups):
            if (r // step) % 2 == phase:
                up = (r + step) % groups
                assert (up // step) % 2 != phase
                perm += [(r, up), (up, r)]
        plans.append((step, phase, step, groups - step, perm))
    return plans


def full_spec(shape):
    return pl.BlockSpec(shape, lambda z: (0,) * len(shape))


def make_local(groups):
    def local(density, momentum, energy):
        planes, rows, count = density.shape
        own, shifts = y_operator(rows, groups)
        weights = np.concatenate([w for _, _, w in shifts], axis=0)
        splits = []
        lo = 0
        for _, _, w in shifts:
            splits.append((lo, lo + w.shape[0]))
            lo += w.shape[0]
        plane_specs = [
            pl.BlockSpec((1, rows, count), lambda z: (z, 0, 0)),
            pl.BlockSpec((3, 1, rows, count), lambda z: (0, z, 0, 0)),
            pl.BlockSpec((1, rows, count), lambda z: (z, 0, 0)),
        ]
        by_shift = {e: (q, split) for (e, q, _), split in zip(shifts, splits)}
        plan = exchange_plan(groups, [e for e, _, _ in shifts])
        index = lax.axis_index("row")
        choices = [(step, phase, first, second) for step, phase, first, second, _ in plan]
        moment_shapes = [
            jax.ShapeDtypeStruct(
                (planes, 5, by_shift[first][1][1] - by_shift[first][1][0], count), jnp.float32
            )
            for _, _, first, _ in choices
        ]
        moment_specs = [
            pl.BlockSpec((1,) + s.shape[1:], lambda z: (z, 0, 0, 0)) for s in moment_shapes
        ]
        split_of = {e: by_shift[e][1] for e in by_shift}
        messages = pl.pallas_call(
            lambda *r: moments_kernel(split_of, choices, *r),
            grid=(planes,),
            in_specs=[pl.BlockSpec(memory_space=pltpu.SMEM), full_spec(weights.shape)]
            + plane_specs,
            out_specs=moment_specs,
            out_shape=moment_shapes,
        )(index.reshape(1).astype(jnp.int32), jnp.asarray(weights), density, momentum, energy)
        received = []
        spreads = []
        for (step, phase, first, second, perm), message in zip(plan, messages):
            received.append(lax.ppermute(message, "row", perm))
            take = ((index // step) % 2 == phase).astype(jnp.float32)
            spreads.append(
                take * jnp.asarray(by_shift[first][0])
                + (1.0 - take) * jnp.asarray(by_shift[second][0])
            )
        spread = jnp.concatenate(spreads, axis=1)
        wx = block_weights(count)
        out_spec = pl.BlockSpec((5, 1, rows, count), lambda z: (0, z, 0, 0))
        out_shape = jax.ShapeDtypeStruct((5, planes, rows, count), jnp.float32)
        partial = pl.pallas_call(
            lambda *r: local_kernel(count, *r),
            grid=(planes,),
            in_specs=[full_spec(wx.shape), full_spec(own.shape)] + plane_specs,
            out_specs=out_spec,
            out_shape=out_shape,
        )(wx, jnp.asarray(own), density, momentum, energy)
        received = jnp.concatenate(received, axis=2)
        return partial - jnp.einsum(
            "pr,zfrx->fzpx", spread, received, precision=HI
        )

    return local


def solution(mesh):
    in_specs = (P("col", "row", None), P(None, "col", "row", None), P("col", "row", None))
    out_specs = P(None, "col", "row", None)
    return jax.shard_map(
        make_local(mesh.shape["row"]),
        mesh=mesh,
        in_specs=in_specs,
        out_specs=out_specs,
        check_vma=False,
    )
```

```python
import jax
import jax.numpy as jnp
import numpy as np
from jax import lax
from jax.experimental import pallas as pl
from jax.experimental.pallas import tpu as pltpu
from jax.sharding import PartitionSpec as P


def operator_column(count):
    steps = np.arange(count)
    wave = 2.0 * np.pi * steps / count
    upper = (
        17.0 / 12.0 * np.sin(wave)
        + 101.0 / 300.0 * np.sin(2.0 * wave)
        + 1.0 / 300.0 * np.sin(3.0 * wave)
    )
    lower = 1.0 + np.cos(wave) + 0.1 * np.cos(2.0 * wave)
    ratio = upper / lower
    phase = 2.0 * np.pi * (steps[:, None] * steps[None, :] % count) / count
    return -np.sum(ratio[:, None] * np.sin(phase), axis=0) / count


def operator_table(count):
    column = operator_column(count)
    steps = np.arange(count)
    offsets = (steps[None, :] - steps[:, None]) % count
    return column[offsets].astype(np.float32)


def block_weights(count):
    table = operator_table(count)
    width = 128
    w_self = table[:width, :width]
    w_prev = table[:width, width : 2 * width]
    w_next = table[width : 2 * width, :width]
    return jnp.asarray(np.concatenate([w_prev, w_self, w_next], axis=1))


def column_basis(block, tol=1e-12):
    rest = block.copy()
    basis = []
    while len(basis) < block.shape[1]:
        norms = np.sqrt(np.sum(rest * rest, axis=0))
        pick = int(np.argmax(norms))
        if norms[pick] <= tol:
            break
        vec = rest[:, pick].copy()
        for _ in range(2):
            for q in basis:
                vec = vec - np.sum(q * vec) * q
        vec = vec / np.sqrt(np.sum(vec * vec))
        basis.append(vec)
        rest = rest - vec[:, None] * np.sum(vec[:, None] * rest, axis=0)[None, :]
    return basis


def y_operator(rows, groups):
    count = rows * groups
    column = operator_column(count)
    steps = np.arange(count)
    full = column[(steps[:, None] - steps[None, :]) % count]
    own = full[:rows, :rows].astype(np.float32)
    shifts = []
    for e in range(1, groups):
        block = full[:rows, rows * e : rows * (e + 1)]
        basis = column_basis(block)
        if not basis:
            continue
        q = np.stack(basis, axis=1)
        w = np.sum(q[:, :, None] * block[:, None, :], axis=0)
        shifts.append((e, q.astype(np.float32), w.astype(np.float32)))
    return own, shifts


HI = lax.Precision.HIGHEST
WIDTH = 128


def dot(a, b):
    return jnp.dot(a, b, precision=HI, preferred_element_type=jnp.float32)


def plane_fluxes(rho_ref, mom_ref, energy_ref):
    rho = rho_ref[0]
    m_x = mom_ref[0, 0]
    m_y = mom_ref[1, 0]
    m_z = mom_ref[2, 0]
    energy = energy_ref[0]
    vel_x = m_x / rho
    vel_y = m_y / rho
    pressure = 0.4 * (energy - 0.5 * (m_x * m_x + m_y * m_y + m_z * m_z) / rho)
    enthalpy = energy + pressure
    flux_x = (m_x, m_x * vel_x + pressure, m_y * vel_x, m_z * vel_x, enthalpy * vel_x)
    flux_y = (m_y, m_x * vel_y, m_y * vel_y + pressure, m_z * vel_y, enthalpy * vel_y)
    return flux_x, flux_y


def moments_kernel(splits, choices, index_ref, weights_ref, rho_ref, mom_ref, energy_ref, *out_refs):
    _, flux_y = plane_fluxes(rho_ref, mom_ref, energy_ref)
    weights = weights_ref[...]
    index = index_ref[0]
    for f in range(5):
        moments = dot(weights, flux_y[f])
        for (step, phase, first, second), out_ref in zip(choices, out_refs):
            pick = (index // step) % 2 != phase
            lo, hi = splits[first]
            lo2, hi2 = splits[second]
            out_ref[0, f] = jnp.where(pick, moments[lo:hi], moments[lo2:hi2])


def local_kernel(count, wx_ref, own_ref, rho_ref, mom_ref, energy_ref, out_ref):
    flux_x, flux_y = plane_fluxes(rho_ref, mom_ref, energy_ref)
    wx = wx_ref[...]
    own = own_ref[...]
    nb = count // WIDTH
    for f in range(5):
        d_y = dot(own, flux_y[f])
        fx = flux_x[f]
        rows = fx.shape[0]
        stacked = jnp.concatenate([fx[:, b * WIDTH : (b + 1) * WIDTH] for b in range(nb)], axis=0)
        parts = dot(stacked, wx)
        for b in range(nb):
            bp = (b - 1) % nb
            bn = (b + 1) % nb
            d_x = (
                parts[bp * rows : (bp + 1) * rows, :WIDTH]
                + parts[b * rows : (b + 1) * rows, WIDTH : 2 * WIDTH]
                + parts[bn * rows : (bn + 1) * rows, 2 * WIDTH :]
            )
            out_ref[f, 0, :, b * WIDTH : (b + 1) * WIDTH] = -(d_x + d_y[:, b * WIDTH : (b + 1) * WIDTH])


def exchange_plan(groups, shift_list):
    assert groups % 4 == 0 and groups >= 8
    assert sorted(shift_list) == sorted({1, 2, groups - 2, groups - 1})
    plans = []
    for step, phase in ((1, 0), (1, 1), (2, 0), (2, 1)):
        perm = []
        for r in range(groups):
            if (r // step) % 2 == phase:
                up = (r + step) % groups
                assert (up // step) % 2 != phase
                perm += [(r, up), (up, r)]
        plans.append((step, phase, step, groups - step, perm))
    return plans


def correct_kernel(spread_ref, partial_ref, *refs):
    recv_refs, out_ref = refs[:-1], refs[-1]
    received = jnp.concatenate([r[0, 0] for r in recv_refs], axis=0)
    out_ref[0, 0] = partial_ref[0, 0] - dot(spread_ref[...], received)


def full_spec(shape):
    return pl.BlockSpec(shape, lambda z: (0,) * len(shape))


def make_local(groups):
    def local(density, momentum, energy):
        planes, rows, count = density.shape
        own, shifts = y_operator(rows, groups)
        weights = np.concatenate([w for _, _, w in shifts], axis=0)
        splits = []
        lo = 0
        for _, _, w in shifts:
            splits.append((lo, lo + w.shape[0]))
            lo += w.shape[0]
        plane_specs = [
            pl.BlockSpec((1, rows, count), lambda z: (z, 0, 0)),
            pl.BlockSpec((3, 1, rows, count), lambda z: (0, z, 0, 0)),
            pl.BlockSpec((1, rows, count), lambda z: (z, 0, 0)),
        ]
        by_shift = {e: (q, split) for (e, q, _), split in zip(shifts, splits)}
        plan = exchange_plan(groups, [e for e, _, _ in shifts])
        index = lax.axis_index("row")
        choices = [(step, phase, first, second) for step, phase, first, second, _ in plan]
        moment_shapes = [
            jax.ShapeDtypeStruct(
                (planes, 5, by_shift[first][1][1] - by_shift[first][1][0], count), jnp.float32
            )
            for _, _, first, _ in choices
        ]
        moment_specs = [
            pl.BlockSpec((1,) + s.shape[1:], lambda z: (z, 0, 0, 0)) for s in moment_shapes
        ]
        split_of = {e: by_shift[e][1] for e in by_shift}
        messages = pl.pallas_call(
            lambda *r: moments_kernel(split_of, choices, *r),
            grid=(planes,),
            in_specs=[pl.BlockSpec(memory_space=pltpu.SMEM), full_spec(weights.shape)]
            + plane_specs,
            out_specs=moment_specs,
            out_shape=moment_shapes,
        )(index.reshape(1).astype(jnp.int32), jnp.asarray(weights), density, momentum, energy)
        received = []
        spreads = []
        for (step, phase, first, second, perm), message in zip(plan, messages):
            received.append(lax.ppermute(message, "row", perm))
            take = ((index // step) % 2 == phase).astype(jnp.float32)
            spreads.append(
                take * jnp.asarray(by_shift[first][0])
                + (1.0 - take) * jnp.asarray(by_shift[second][0])
            )
        spread = jnp.concatenate(spreads, axis=1)
        wx = block_weights(count)
        out_spec = pl.BlockSpec((5, 1, rows, count), lambda z: (0, z, 0, 0))
        out_shape = jax.ShapeDtypeStruct((5, planes, rows, count), jnp.float32)
        partial = pl.pallas_call(
            lambda *r: local_kernel(count, *r),
            grid=(planes,),
            in_specs=[full_spec(wx.shape), full_spec(own.shape)] + plane_specs,
            out_specs=out_spec,
            out_shape=out_shape,
        )(wx, jnp.asarray(own), density, momentum, energy)
        field_spec = pl.BlockSpec((1, 1, rows, count), lambda z, f: (f, z, 0, 0))
        return pl.pallas_call(
            correct_kernel,
            grid=(planes, 5),
            in_specs=[pl.BlockSpec(spread.shape, lambda z, f: (0, 0)), field_spec]
            + [pl.BlockSpec((1, 1) + r.shape[2:], lambda z, f: (z, f, 0, 0)) for r in received],
            out_specs=field_spec,
            out_shape=out_shape,
            input_output_aliases={1: 0},
        )(spread, partial, *received)

    return local


def solution(mesh):
    in_specs = (P("col", "row", None), P(None, "col", "row", None), P("col", "row", None))
    out_specs = P(None, "col", "row", None)
    return jax.shard_map(
        make_local(mesh.shape["row"]),
        mesh=mesh,
        in_specs=in_specs,
        out_specs=out_specs,
        check_vma=False,
    )
```

```python
import jax
import jax.numpy as jnp
import numpy as np
from jax import lax
from jax.experimental import pallas as pl
from jax.experimental.pallas import tpu as pltpu
from jax.sharding import PartitionSpec as P


def operator_column(count):
    steps = np.arange(count)
    wave = 2.0 * np.pi * steps / count
    upper = (
        17.0 / 12.0 * np.sin(wave)
        + 101.0 / 300.0 * np.sin(2.0 * wave)
        + 1.0 / 300.0 * np.sin(3.0 * wave)
    )
    lower = 1.0 + np.cos(wave) + 0.1 * np.cos(2.0 * wave)
    ratio = upper / lower
    phase = 2.0 * np.pi * (steps[:, None] * steps[None, :] % count) / count
    return -np.sum(ratio[:, None] * np.sin(phase), axis=0) / count


def operator_table(count):
    column = operator_column(count)
    steps = np.arange(count)
    offsets = (steps[None, :] - steps[:, None]) % count
    return column[offsets].astype(np.float32)


def block_weights(count):
    table = operator_table(count)
    width = 128
    w_self = table[:width, :width]
    w_prev = table[:width, width : 2 * width]
    w_next = table[width : 2 * width, :width]
    return jnp.asarray(np.concatenate([w_prev, w_self, w_next], axis=1))


def column_basis(block, tol=1e-12):
    rest = block.copy()
    basis = []
    while len(basis) < block.shape[1]:
        norms = np.sqrt(np.sum(rest * rest, axis=0))
        pick = int(np.argmax(norms))
        if norms[pick] <= tol:
            break
        vec = rest[:, pick].copy()
        for _ in range(2):
            for q in basis:
                vec = vec - np.sum(q * vec) * q
        vec = vec / np.sqrt(np.sum(vec * vec))
        basis.append(vec)
        rest = rest - vec[:, None] * np.sum(vec[:, None] * rest, axis=0)[None, :]
    return basis


def y_operator(rows, groups):
    count = rows * groups
    column = operator_column(count)
    steps = np.arange(count)
    full = column[(steps[:, None] - steps[None, :]) % count]
    own = full[:rows, :rows].astype(np.float32)
    shifts = []
    for e in range(1, groups):
        block = full[:rows, rows * e : rows * (e + 1)]
        basis = column_basis(block)
        if not basis:
            continue
        q = np.stack(basis, axis=1)
        w = np.sum(q[:, :, None] * block[:, None, :], axis=0)
        shifts.append((e, q.astype(np.float32), w.astype(np.float32)))
    return own, shifts


HI = lax.Precision.HIGHEST
WIDTH = 128


def dot(a, b):
    return jnp.dot(a, b, precision=HI, preferred_element_type=jnp.float32)


def plane_fluxes(rho_ref, mom_ref, energy_ref):
    rho = rho_ref[0]
    m_x = mom_ref[0, 0]
    m_y = mom_ref[1, 0]
    m_z = mom_ref[2, 0]
    energy = energy_ref[0]
    vel_x = m_x / rho
    vel_y = m_y / rho
    pressure = 0.4 * (energy - 0.5 * (m_x * m_x + m_y * m_y + m_z * m_z) / rho)
    enthalpy = energy + pressure
    flux_x = (m_x, m_x * vel_x + pressure, m_y * vel_x, m_z * vel_x, enthalpy * vel_x)
    flux_y = (m_y, m_x * vel_y, m_y * vel_y + pressure, m_z * vel_y, enthalpy * vel_y)
    return flux_x, flux_y


def moments_kernel(splits, choices, index_ref, weights_ref, rho_ref, mom_ref, energy_ref, *out_refs):
    _, flux_y = plane_fluxes(rho_ref, mom_ref, energy_ref)
    weights = weights_ref[...]
    index = index_ref[0]
    for f in range(5):
        moments = dot(weights, flux_y[f])
        for (step, phase, first, second), out_ref in zip(choices, out_refs):
            pick = (index // step) % 2 != phase
            lo, hi = splits[first]
            lo2, hi2 = splits[second]
            out_ref[0, f] = jnp.where(pick, moments[lo:hi], moments[lo2:hi2])


def local_kernel(count, wx_ref, own_ref, rho_ref, mom_ref, energy_ref, out_ref):
    flux_x, flux_y = plane_fluxes(rho_ref, mom_ref, energy_ref)
    wx = wx_ref[...]
    own = own_ref[...]
    nb = count // WIDTH
    d_all = dot(own, jnp.concatenate(flux_y, axis=1))
    for f in range(5):
        d_y = d_all[:, f * count : (f + 1) * count]
        fx = flux_x[f]
        rows = fx.shape[0]
        stacked = jnp.concatenate([fx[:, b * WIDTH : (b + 1) * WIDTH] for b in range(nb)], axis=0)
        parts = dot(stacked, wx)
        for b in range(nb):
            bp = (b - 1) % nb
            bn = (b + 1) % nb
            d_x = (
                parts[bp * rows : (bp + 1) * rows, :WIDTH]
                + parts[b * rows : (b + 1) * rows, WIDTH : 2 * WIDTH]
                + parts[bn * rows : (bn + 1) * rows, 2 * WIDTH :]
            )
            out_ref[f, 0, :, b * WIDTH : (b + 1) * WIDTH] = -(d_x + d_y[:, b * WIDTH : (b + 1) * WIDTH])


def exchange_plan(groups, shift_list):
    assert groups % 4 == 0 and groups >= 8
    assert sorted(shift_list) == sorted({1, 2, groups - 2, groups - 1})
    plans = []
    for step, phase in ((1, 0), (1, 1), (2, 0), (2, 1)):
        perm = []
        for r in range(groups):
            if (r // step) % 2 == phase:
                up = (r + step) % groups
                assert (up // step) % 2 != phase
                perm += [(r, up), (up, r)]
        plans.append((step, phase, step, groups - step, perm))
    return plans


def full_spec(shape):
    return pl.BlockSpec(shape, lambda z: (0,) * len(shape))


def make_local(groups):
    def local(density, momentum, energy):
        planes, rows, count = density.shape
        own, shifts = y_operator(rows, groups)
        weights = np.concatenate([w for _, _, w in shifts], axis=0)
        splits = []
        lo = 0
        for _, _, w in shifts:
            splits.append((lo, lo + w.shape[0]))
            lo += w.shape[0]
        plane_specs = [
            pl.BlockSpec((1, rows, count), lambda z: (z, 0, 0)),
            pl.BlockSpec((3, 1, rows, count), lambda z: (0, z, 0, 0)),
            pl.BlockSpec((1, rows, count), lambda z: (z, 0, 0)),
        ]
        by_shift = {e: (q, split) for (e, q, _), split in zip(shifts, splits)}
        plan = exchange_plan(groups, [e for e, _, _ in shifts])
        index = lax.axis_index("row")
        choices = [(step, phase, first, second) for step, phase, first, second, _ in plan]
        moment_shapes = [
            jax.ShapeDtypeStruct(
                (planes, 5, by_shift[first][1][1] - by_shift[first][1][0], count), jnp.float32
            )
            for _, _, first, _ in choices
        ]
        moment_specs = [
            pl.BlockSpec((1,) + s.shape[1:], lambda z: (z, 0, 0, 0)) for s in moment_shapes
        ]
        split_of = {e: by_shift[e][1] for e in by_shift}
        messages = pl.pallas_call(
            lambda *r: moments_kernel(split_of, choices, *r),
            grid=(planes,),
            in_specs=[pl.BlockSpec(memory_space=pltpu.SMEM), full_spec(weights.shape)]
            + plane_specs,
            out_specs=moment_specs,
            out_shape=moment_shapes,
        )(index.reshape(1).astype(jnp.int32), jnp.asarray(weights), density, momentum, energy)
        received = []
        spreads = []
        for (step, phase, first, second, perm), message in zip(plan, messages):
            received.append(lax.ppermute(message, "row", perm))
            take = ((index // step) % 2 == phase).astype(jnp.float32)
            spreads.append(
                take * jnp.asarray(by_shift[first][0])
                + (1.0 - take) * jnp.asarray(by_shift[second][0])
            )
        spread = jnp.concatenate(spreads, axis=1)
        wx = block_weights(count)
        out_spec = pl.BlockSpec((5, 1, rows, count), lambda z: (0, z, 0, 0))
        out_shape = jax.ShapeDtypeStruct((5, planes, rows, count), jnp.float32)
        partial = pl.pallas_call(
            lambda *r: local_kernel(count, *r),
            grid=(planes,),
            in_specs=[full_spec(wx.shape), full_spec(own.shape)] + plane_specs,
            out_specs=out_spec,
            out_shape=out_shape,
        )(wx, jnp.asarray(own), density, momentum, energy)
        received = jnp.concatenate(received, axis=2)
        return partial - jnp.einsum(
            "pr,zfrx->fzpx", spread, received, precision=HI
        )

    return local


def solution(mesh):
    in_specs = (P("col", "row", None), P(None, "col", "row", None), P("col", "row", None))
    out_specs = P(None, "col", "row", None)
    return jax.shard_map(
        make_local(mesh.shape["row"]),
        mesh=mesh,
        in_specs=in_specs,
        out_specs=out_specs,
        check_vma=False,
    )
```

```python
import jax
import jax.numpy as jnp
import numpy as np
from jax import lax
from jax.experimental import pallas as pl
from jax.experimental.pallas import tpu as pltpu
from jax.sharding import PartitionSpec as P


def operator_column(count):
    steps = np.arange(count)
    wave = 2.0 * np.pi * steps / count
    upper = (
        17.0 / 12.0 * np.sin(wave)
        + 101.0 / 300.0 * np.sin(2.0 * wave)
        + 1.0 / 300.0 * np.sin(3.0 * wave)
    )
    lower = 1.0 + np.cos(wave) + 0.1 * np.cos(2.0 * wave)
    ratio = upper / lower
    phase = 2.0 * np.pi * (steps[:, None] * steps[None, :] % count) / count
    return -np.sum(ratio[:, None] * np.sin(phase), axis=0) / count


def operator_table(count):
    column = operator_column(count)
    steps = np.arange(count)
    offsets = (steps[None, :] - steps[:, None]) % count
    return column[offsets].astype(np.float32)


def block_weights(count):
    table = operator_table(count)
    width = 128
    w_self = table[:width, :width]
    w_prev = table[:width, width : 2 * width]
    w_next = table[width : 2 * width, :width]
    return jnp.asarray(np.concatenate([w_prev, w_self, w_next], axis=1))


def column_basis(block, tol=1e-12):
    rest = block.copy()
    basis = []
    while len(basis) < block.shape[1]:
        norms = np.sqrt(np.sum(rest * rest, axis=0))
        pick = int(np.argmax(norms))
        if norms[pick] <= tol:
            break
        vec = rest[:, pick].copy()
        for _ in range(2):
            for q in basis:
                vec = vec - np.sum(q * vec) * q
        vec = vec / np.sqrt(np.sum(vec * vec))
        basis.append(vec)
        rest = rest - vec[:, None] * np.sum(vec[:, None] * rest, axis=0)[None, :]
    return basis


def y_operator(rows, groups):
    count = rows * groups
    column = operator_column(count)
    steps = np.arange(count)
    full = column[(steps[:, None] - steps[None, :]) % count]
    own = full[:rows, :rows].astype(np.float32)
    shifts = []
    for e in range(1, groups):
        block = full[:rows, rows * e : rows * (e + 1)]
        basis = column_basis(block)
        if not basis:
            continue
        q = np.stack(basis, axis=1)
        w = np.sum(q[:, :, None] * block[:, None, :], axis=0)
        shifts.append((e, q.astype(np.float32), w.astype(np.float32)))
    return own, shifts


HI = lax.Precision.HIGHEST
WIDTH = 128


def dot(a, b):
    return jnp.dot(a, b, precision=HI, preferred_element_type=jnp.float32)


def plane_fluxes(rho_ref, mom_ref, energy_ref):
    rho = rho_ref[0]
    m_x = mom_ref[0, 0]
    m_y = mom_ref[1, 0]
    m_z = mom_ref[2, 0]
    energy = energy_ref[0]
    vel_x = m_x / rho
    vel_y = m_y / rho
    pressure = 0.4 * (energy - 0.5 * (m_x * m_x + m_y * m_y + m_z * m_z) / rho)
    enthalpy = energy + pressure
    flux_x = (m_x, m_x * vel_x + pressure, m_y * vel_x, m_z * vel_x, enthalpy * vel_x)
    flux_y = (m_y, m_x * vel_y, m_y * vel_y + pressure, m_z * vel_y, enthalpy * vel_y)
    return flux_x, flux_y


def moments_kernel(splits, choices, index_ref, weights_ref, rho_ref, mom_ref, energy_ref, *out_refs):
    _, flux_y = plane_fluxes(rho_ref, mom_ref, energy_ref)
    weights = weights_ref[...]
    index = index_ref[0]
    for f in range(5):
        moments = dot(weights, flux_y[f])
        for (step, phase, first, second), out_ref in zip(choices, out_refs):
            pick = (index // step) % 2 != phase
            lo, hi = splits[first]
            lo2, hi2 = splits[second]
            out_ref[0, f] = jnp.where(pick, moments[lo:hi], moments[lo2:hi2])


def local_kernel(
    count, wx_ref, own_ref, rho_hbm, mom_hbm, energy_hbm, out_hbm,
    rho_v, mom_v, energy_v, out_v, in_sem, out_sem,
):
    z = pl.program_id(0)
    plane = pl.ds(z, 1)
    loads = [
        pltpu.make_async_copy(mom_hbm.at[0, plane], mom_v.at[0], in_sem.at[0]),
        pltpu.make_async_copy(mom_hbm.at[1, plane], mom_v.at[1], in_sem.at[1]),
        pltpu.make_async_copy(rho_hbm.at[plane], rho_v, in_sem.at[2]),
        pltpu.make_async_copy(mom_hbm.at[2, plane], mom_v.at[2], in_sem.at[3]),
        pltpu.make_async_copy(energy_hbm.at[plane], energy_v, in_sem.at[4]),
    ]
    for copy in loads:
        copy.start()
    wx = wx_ref[...]
    own = own_ref[...]
    nb = count // WIDTH
    stores = []

    def emit(f, fx, fy):
        d_y = dot(own, fy)
        rows = fx.shape[0]
        stacked = jnp.concatenate([fx[:, b * WIDTH : (b + 1) * WIDTH] for b in range(nb)], axis=0)
        parts = dot(stacked, wx)
        for b in range(nb):
            bp = (b - 1) % nb
            bn = (b + 1) % nb
            d_x = (
                parts[bp * rows : (bp + 1) * rows, :WIDTH]
                + parts[b * rows : (b + 1) * rows, WIDTH : 2 * WIDTH]
                + parts[bn * rows : (bn + 1) * rows, 2 * WIDTH :]
            )
            out_v[f, 0, :, b * WIDTH : (b + 1) * WIDTH] = -(d_x + d_y[:, b * WIDTH : (b + 1) * WIDTH])
        store = pltpu.make_async_copy(out_v.at[f], out_hbm.at[f, plane], out_sem.at[f])
        store.start()
        stores.append(store)

    loads[0].wait()
    loads[1].wait()
    emit(0, mom_v[0, 0], mom_v[1, 0])
    for copy in loads[2:]:
        copy.wait()
    flux_x, flux_y = plane_fluxes(rho_v, mom_v, energy_v)
    for f in range(1, 5):
        emit(f, flux_x[f], flux_y[f])
    for store in stores:
        store.wait()


def exchange_plan(groups, shift_list):
    assert groups % 4 == 0 and groups >= 8
    assert sorted(shift_list) == sorted({1, 2, groups - 2, groups - 1})
    plans = []
    for step, phase in ((1, 0), (1, 1), (2, 0), (2, 1)):
        perm = []
        for r in range(groups):
            if (r // step) % 2 == phase:
                up = (r + step) % groups
                assert (up // step) % 2 != phase
                perm += [(r, up), (up, r)]
        plans.append((step, phase, step, groups - step, perm))
    return plans


def full_spec(shape):
    return pl.BlockSpec(shape, lambda z: (0,) * len(shape))


def make_local(groups):
    def local(density, momentum, energy):
        planes, rows, count = density.shape
        own, shifts = y_operator(rows, groups)
        weights = np.concatenate([w for _, _, w in shifts], axis=0)
        splits = []
        lo = 0
        for _, _, w in shifts:
            splits.append((lo, lo + w.shape[0]))
            lo += w.shape[0]
        plane_specs = [
            pl.BlockSpec((1, rows, count), lambda z: (z, 0, 0)),
            pl.BlockSpec((3, 1, rows, count), lambda z: (0, z, 0, 0)),
            pl.BlockSpec((1, rows, count), lambda z: (z, 0, 0)),
        ]
        by_shift = {e: (q, split) for (e, q, _), split in zip(shifts, splits)}
        plan = exchange_plan(groups, [e for e, _, _ in shifts])
        index = lax.axis_index("row")
        choices = [(step, phase, first, second) for step, phase, first, second, _ in plan]
        moment_shapes = [
            jax.ShapeDtypeStruct(
                (planes, 5, by_shift[first][1][1] - by_shift[first][1][0], count), jnp.float32
            )
            for _, _, first, _ in choices
        ]
        moment_specs = [
            pl.BlockSpec((1,) + s.shape[1:], lambda z: (z, 0, 0, 0)) for s in moment_shapes
        ]
        split_of = {e: by_shift[e][1] for e in by_shift}
        messages = pl.pallas_call(
            lambda *r: moments_kernel(split_of, choices, *r),
            grid=(planes,),
            in_specs=[pl.BlockSpec(memory_space=pltpu.SMEM), full_spec(weights.shape)]
            + plane_specs,
            out_specs=moment_specs,
            out_shape=moment_shapes,
        )(index.reshape(1).astype(jnp.int32), jnp.asarray(weights), density, momentum, energy)
        received = []
        spreads = []
        for (step, phase, first, second, perm), message in zip(plan, messages):
            received.append(lax.ppermute(message, "row", perm))
            take = ((index // step) % 2 == phase).astype(jnp.float32)
            spreads.append(
                take * jnp.asarray(by_shift[first][0])
                + (1.0 - take) * jnp.asarray(by_shift[second][0])
            )
        spread = jnp.concatenate(spreads, axis=1)
        wx = block_weights(count)
        out_spec = pl.BlockSpec((5, 1, rows, count), lambda z: (0, z, 0, 0))
        out_shape = jax.ShapeDtypeStruct((5, planes, rows, count), jnp.float32)
        hbm = pl.BlockSpec(memory_space=pl.ANY)
        partial = pl.pallas_call(
            lambda *r: local_kernel(count, *r),
            grid=(planes,),
            in_specs=[full_spec(wx.shape), full_spec(own.shape), hbm, hbm, hbm],
            out_specs=hbm,
            out_shape=out_shape,
            scratch_shapes=[
                pltpu.VMEM((1, rows, count), jnp.float32),
                pltpu.VMEM((3, 1, rows, count), jnp.float32),
                pltpu.VMEM((1, rows, count), jnp.float32),
                pltpu.VMEM((5, 1, rows, count), jnp.float32),
                pltpu.SemaphoreType.DMA((5,)),
                pltpu.SemaphoreType.DMA((5,)),
            ],
        )(wx, jnp.asarray(own), density, momentum, energy)
        received = jnp.concatenate(received, axis=2)
        return partial - jnp.einsum(
            "pr,zfrx->fzpx", spread, received, precision=HI
        )

    return local


def solution(mesh):
    in_specs = (P("col", "row", None), P(None, "col", "row", None), P("col", "row", None))
    out_specs = P(None, "col", "row", None)
    return jax.shard_map(
        make_local(mesh.shape["row"]),
        mesh=mesh,
        in_specs=in_specs,
        out_specs=out_specs,
        check_vma=False,
    )
```

```python
import jax
import jax.numpy as jnp
import numpy as np
from jax import lax
from jax.experimental import pallas as pl
from jax.experimental.pallas import tpu as pltpu
from jax.sharding import PartitionSpec as P


def operator_column(count):
    steps = np.arange(count)
    wave = 2.0 * np.pi * steps / count
    upper = (
        17.0 / 12.0 * np.sin(wave)
        + 101.0 / 300.0 * np.sin(2.0 * wave)
        + 1.0 / 300.0 * np.sin(3.0 * wave)
    )
    lower = 1.0 + np.cos(wave) + 0.1 * np.cos(2.0 * wave)
    ratio = upper / lower
    phase = 2.0 * np.pi * (steps[:, None] * steps[None, :] % count) / count
    return -np.sum(ratio[:, None] * np.sin(phase), axis=0) / count


def operator_table(count):
    column = operator_column(count)
    steps = np.arange(count)
    offsets = (steps[None, :] - steps[:, None]) % count
    return column[offsets].astype(np.float32)


def block_weights(count):
    table = operator_table(count)
    width = 128
    w_self = table[:width, :width]
    w_prev = table[:width, width : 2 * width]
    w_next = table[width : 2 * width, :width]
    return jnp.asarray(np.concatenate([w_prev, w_self, w_next], axis=1))


def column_basis(block, tol=1e-12):
    rest = block.copy()
    basis = []
    while len(basis) < block.shape[1]:
        norms = np.sqrt(np.sum(rest * rest, axis=0))
        pick = int(np.argmax(norms))
        if norms[pick] <= tol:
            break
        vec = rest[:, pick].copy()
        for _ in range(2):
            for q in basis:
                vec = vec - np.sum(q * vec) * q
        vec = vec / np.sqrt(np.sum(vec * vec))
        basis.append(vec)
        rest = rest - vec[:, None] * np.sum(vec[:, None] * rest, axis=0)[None, :]
    return basis


def y_operator(rows, groups):
    count = rows * groups
    column = operator_column(count)
    steps = np.arange(count)
    full = column[(steps[:, None] - steps[None, :]) % count]
    own = full[:rows, :rows].astype(np.float32)
    shifts = []
    for e in range(1, groups):
        block = full[:rows, rows * e : rows * (e + 1)]
        basis = column_basis(block)
        if not basis:
            continue
        q = np.stack(basis, axis=1)
        w = np.sum(q[:, :, None] * block[:, None, :], axis=0)
        shifts.append((e, q.astype(np.float32), w.astype(np.float32)))
    return own, shifts


HI = lax.Precision.HIGHEST
WIDTH = 128


def dot(a, b):
    return jnp.dot(a, b, precision=HI, preferred_element_type=jnp.float32)


def plane_fluxes(rho_ref, mom_ref, energy_ref):
    rho = rho_ref[0]
    m_x = mom_ref[0, 0]
    m_y = mom_ref[1, 0]
    m_z = mom_ref[2, 0]
    energy = energy_ref[0]
    vel_x = m_x / rho
    vel_y = m_y / rho
    pressure = 0.4 * (energy - 0.5 * (m_x * m_x + m_y * m_y + m_z * m_z) / rho)
    enthalpy = energy + pressure
    flux_x = (m_x, m_x * vel_x + pressure, m_y * vel_x, m_z * vel_x, enthalpy * vel_x)
    flux_y = (m_y, m_x * vel_y, m_y * vel_y + pressure, m_z * vel_y, enthalpy * vel_y)
    return flux_x, flux_y


def moments_kernel(
    splits, choices, index_ref, weights_ref, rho_hbm, mom_hbm, energy_hbm, *refs
):
    out_refs = refs[: len(choices)]
    rho_v, mom_v, energy_v, in_sem = refs[len(choices) :]
    z = pl.program_id(0)
    plane = pl.ds(z, 1)
    loads = [
        pltpu.make_async_copy(mom_hbm.at[1, plane], mom_v.at[1], in_sem.at[0]),
        pltpu.make_async_copy(rho_hbm.at[plane], rho_v, in_sem.at[1]),
        pltpu.make_async_copy(mom_hbm.at[0, plane], mom_v.at[0], in_sem.at[2]),
        pltpu.make_async_copy(mom_hbm.at[2, plane], mom_v.at[2], in_sem.at[3]),
        pltpu.make_async_copy(energy_hbm.at[plane], energy_v, in_sem.at[4]),
    ]
    for copy in loads:
        copy.start()
    weights = weights_ref[...]
    index = index_ref[0]

    def emit(f, fy):
        moments = dot(weights, fy)
        for (step, phase, first, second), out_ref in zip(choices, out_refs):
            pick = (index // step) % 2 != phase
            lo, hi = splits[first]
            lo2, hi2 = splits[second]
            out_ref[0, f] = jnp.where(pick, moments[lo:hi], moments[lo2:hi2])

    loads[0].wait()
    emit(0, mom_v[1, 0])
    loads[1].wait()
    loads[2].wait()
    rho = rho_v[0]
    m_x = mom_v[0, 0]
    m_y = mom_v[1, 0]
    vel_y = m_y / rho
    emit(1, m_x * vel_y)
    loads[3].wait()
    loads[4].wait()
    _, flux_y = plane_fluxes(rho_v, mom_v, energy_v)
    for f in range(2, 5):
        emit(f, flux_y[f])


def local_kernel(count, wx_ref, own_ref, rho_ref, mom_ref, energy_ref, out_ref):
    flux_x, flux_y = plane_fluxes(rho_ref, mom_ref, energy_ref)
    wx = wx_ref[...]
    own = own_ref[...]
    nb = count // WIDTH
    d_all = dot(own, jnp.concatenate(flux_y, axis=1))
    for f in range(5):
        d_y = d_all[:, f * count : (f + 1) * count]
        fx = flux_x[f]
        rows = fx.shape[0]
        stacked = jnp.concatenate([fx[:, b * WIDTH : (b + 1) * WIDTH] for b in range(nb)], axis=0)
        parts = dot(stacked, wx)
        for b in range(nb):
            bp = (b - 1) % nb
            bn = (b + 1) % nb
            d_x = (
                parts[bp * rows : (bp + 1) * rows, :WIDTH]
                + parts[b * rows : (b + 1) * rows, WIDTH : 2 * WIDTH]
                + parts[bn * rows : (bn + 1) * rows, 2 * WIDTH :]
            )
            out_ref[f, 0, :, b * WIDTH : (b + 1) * WIDTH] = -(d_x + d_y[:, b * WIDTH : (b + 1) * WIDTH])


def exchange_plan(groups, shift_list):
    assert groups % 4 == 0 and groups >= 8
    assert sorted(shift_list) == sorted({1, 2, groups - 2, groups - 1})
    plans = []
    for step, phase in ((1, 0), (1, 1), (2, 0), (2, 1)):
        perm = []
        for r in range(groups):
            if (r // step) % 2 == phase:
                up = (r + step) % groups
                assert (up // step) % 2 != phase
                perm += [(r, up), (up, r)]
        plans.append((step, phase, step, groups - step, perm))
    return plans


def full_spec(shape):
    return pl.BlockSpec(shape, lambda z: (0,) * len(shape))


def make_local(groups):
    def local(density, momentum, energy):
        planes, rows, count = density.shape
        own, shifts = y_operator(rows, groups)
        weights = np.concatenate([w for _, _, w in shifts], axis=0)
        splits = []
        lo = 0
        for _, _, w in shifts:
            splits.append((lo, lo + w.shape[0]))
            lo += w.shape[0]
        plane_specs = [
            pl.BlockSpec((1, rows, count), lambda z: (z, 0, 0)),
            pl.BlockSpec((3, 1, rows, count), lambda z: (0, z, 0, 0)),
            pl.BlockSpec((1, rows, count), lambda z: (z, 0, 0)),
        ]
        by_shift = {e: (q, split) for (e, q, _), split in zip(shifts, splits)}
        plan = exchange_plan(groups, [e for e, _, _ in shifts])
        index = lax.axis_index("row")
        choices = [(step, phase, first, second) for step, phase, first, second, _ in plan]
        moment_shapes = [
            jax.ShapeDtypeStruct(
                (planes, 5, by_shift[first][1][1] - by_shift[first][1][0], count), jnp.float32
            )
            for _, _, first, _ in choices
        ]
        moment_specs = [
            pl.BlockSpec((1,) + s.shape[1:], lambda z: (z, 0, 0, 0)) for s in moment_shapes
        ]
        split_of = {e: by_shift[e][1] for e in by_shift}
        messages = pl.pallas_call(
            lambda *r: moments_kernel(split_of, choices, *r),
            grid=(planes,),
            in_specs=[pl.BlockSpec(memory_space=pltpu.SMEM), full_spec(weights.shape)]
            + [pl.BlockSpec(memory_space=pl.ANY)] * 3,
            out_specs=moment_specs,
            out_shape=moment_shapes,
            scratch_shapes=[
                pltpu.VMEM((1, rows, count), jnp.float32),
                pltpu.VMEM((3, 1, rows, count), jnp.float32),
                pltpu.VMEM((1, rows, count), jnp.float32),
                pltpu.SemaphoreType.DMA((5,)),
            ],
        )(index.reshape(1).astype(jnp.int32), jnp.asarray(weights), density, momentum, energy)
        received = []
        spreads = []
        for (step, phase, first, second, perm), message in zip(plan, messages):
            received.append(lax.ppermute(message, "row", perm))
            take = ((index // step) % 2 == phase).astype(jnp.float32)
            spreads.append(
                take * jnp.asarray(by_shift[first][0])
                + (1.0 - take) * jnp.asarray(by_shift[second][0])
            )
        spread = jnp.concatenate(spreads, axis=1)
        wx = block_weights(count)
        out_spec = pl.BlockSpec((5, 1, rows, count), lambda z: (0, z, 0, 0))
        out_shape = jax.ShapeDtypeStruct((5, planes, rows, count), jnp.float32)
        partial = pl.pallas_call(
            lambda *r: local_kernel(count, *r),
            grid=(planes,),
            in_specs=[full_spec(wx.shape), full_spec(own.shape)] + plane_specs,
            out_specs=out_spec,
            out_shape=out_shape,
        )(wx, jnp.asarray(own), density, momentum, energy)
        received = jnp.concatenate(received, axis=2)
        return partial - jnp.einsum(
            "pr,zfrx->fzpx", spread, received, precision=HI
        )

    return local


def solution(mesh):
    in_specs = (P("col", "row", None), P(None, "col", "row", None), P("col", "row", None))
    out_specs = P(None, "col", "row", None)
    return jax.shard_map(
        make_local(mesh.shape["row"]),
        mesh=mesh,
        in_specs=in_specs,
        out_specs=out_specs,
        check_vma=False,
    )
```

```python
import jax
import jax.numpy as jnp
import numpy as np
from jax import lax
from jax.experimental import pallas as pl
from jax.experimental.pallas import tpu as pltpu
from jax.sharding import PartitionSpec as P


def operator_column(count):
    steps = np.arange(count)
    wave = 2.0 * np.pi * steps / count
    upper = (
        17.0 / 12.0 * np.sin(wave)
        + 101.0 / 300.0 * np.sin(2.0 * wave)
        + 1.0 / 300.0 * np.sin(3.0 * wave)
    )
    lower = 1.0 + np.cos(wave) + 0.1 * np.cos(2.0 * wave)
    ratio = upper / lower
    phase = 2.0 * np.pi * (steps[:, None] * steps[None, :] % count) / count
    return -np.sum(ratio[:, None] * np.sin(phase), axis=0) / count


def operator_table(count):
    column = operator_column(count)
    steps = np.arange(count)
    offsets = (steps[None, :] - steps[:, None]) % count
    return column[offsets].astype(np.float32)


def block_weights(count):
    table = operator_table(count)
    width = 128
    w_self = table[:width, :width]
    w_prev = table[:width, width : 2 * width]
    w_next = table[width : 2 * width, :width]
    return jnp.asarray(np.concatenate([w_prev, w_self, w_next], axis=1))


def column_basis(block, tol=1e-12):
    rest = block.copy()
    basis = []
    while len(basis) < block.shape[1]:
        norms = np.sqrt(np.sum(rest * rest, axis=0))
        pick = int(np.argmax(norms))
        if norms[pick] <= tol:
            break
        vec = rest[:, pick].copy()
        for _ in range(2):
            for q in basis:
                vec = vec - np.sum(q * vec) * q
        vec = vec / np.sqrt(np.sum(vec * vec))
        basis.append(vec)
        rest = rest - vec[:, None] * np.sum(vec[:, None] * rest, axis=0)[None, :]
    return basis


def y_operator(rows, groups):
    count = rows * groups
    column = operator_column(count)
    steps = np.arange(count)
    full = column[(steps[:, None] - steps[None, :]) % count]
    own = full[:rows, :rows].astype(np.float32)
    shifts = []
    for e in range(1, groups):
        block = full[:rows, rows * e : rows * (e + 1)]
        basis = column_basis(block)
        if not basis:
            continue
        q = np.stack(basis, axis=1)
        w = np.sum(q[:, :, None] * block[:, None, :], axis=0)
        shifts.append((e, q.astype(np.float32), w.astype(np.float32)))
    return own, shifts


HI = lax.Precision.HIGHEST
WIDTH = 128


def dot(a, b):
    return jnp.dot(a, b, precision=HI, preferred_element_type=jnp.float32)


def plane_fluxes(rho_ref, mom_ref, energy_ref):
    rho = rho_ref[0]
    m_x = mom_ref[0, 0]
    m_y = mom_ref[1, 0]
    m_z = mom_ref[2, 0]
    energy = energy_ref[0]
    vel_x = m_x / rho
    vel_y = m_y / rho
    pressure = 0.4 * (energy - 0.5 * (m_x * m_x + m_y * m_y + m_z * m_z) / rho)
    enthalpy = energy + pressure
    flux_x = (m_x, m_x * vel_x + pressure, m_y * vel_x, m_z * vel_x, enthalpy * vel_x)
    flux_y = (m_y, m_x * vel_y, m_y * vel_y + pressure, m_z * vel_y, enthalpy * vel_y)
    return flux_x, flux_y


def moments_kernel(splits, choices, index_ref, weights_ref, rho_ref, mom_ref, energy_ref, *out_refs):
    _, flux_y = plane_fluxes(rho_ref, mom_ref, energy_ref)
    weights = weights_ref[...]
    index = index_ref[0]
    for f in range(5):
        moments = dot(weights, flux_y[f])
        for (step, phase, first, second), out_ref in zip(choices, out_refs):
            pick = (index // step) % 2 != phase
            lo, hi = splits[first]
            lo2, hi2 = splits[second]
            out_ref[0, f] = jnp.where(pick, moments[lo:hi], moments[lo2:hi2])


def field_tendency(count, wx, own, flux_x, flux_y, fields):
    nb = count // WIDTH
    d_all = dot(own, jnp.concatenate([flux_y[f] for f in fields], axis=1))
    results = []
    for i, f in enumerate(fields):
        fx = flux_x[f]
        rows = fx.shape[0]
        stacked = jnp.concatenate([fx[:, b * WIDTH : (b + 1) * WIDTH] for b in range(nb)], axis=0)
        parts = dot(stacked, wx)
        pieces = []
        for b in range(nb):
            bp = (b - 1) % nb
            bn = (b + 1) % nb
            d_x = (
                parts[bp * rows : (bp + 1) * rows, :WIDTH]
                + parts[b * rows : (b + 1) * rows, WIDTH : 2 * WIDTH]
                + parts[bn * rows : (bn + 1) * rows, 2 * WIDTH :]
            )
            lo = i * count + b * WIDTH
            pieces.append(-(d_x + d_all[:, lo : lo + WIDTH]))
        results.append(pieces)
    return results


def local_kernel(count, fields, wx_ref, own_ref, rho_ref, mom_ref, energy_ref, out_ref):
    flux_x, flux_y = plane_fluxes(rho_ref, mom_ref, energy_ref)
    results = field_tendency(count, wx_ref[...], own_ref[...], flux_x, flux_y, fields)
    for i, pieces in enumerate(results):
        for b, piece in enumerate(pieces):
            out_ref[i, 0, :, b * WIDTH : (b + 1) * WIDTH] = piece


def final_kernel(count, early, late, wx_ref, own_ref, spread_ref, rho_ref, mom_ref, energy_ref, partial_ref, *refs):
    recv_refs, out_ref = refs[:-1], refs[-1]
    spread = spread_ref[...]

    def correction(f):
        received = jnp.concatenate([r[0, f] for r in recv_refs], axis=0)
        return dot(spread, received)

    for i, f in enumerate(early):
        out_ref[f, 0] = partial_ref[i, 0] - correction(f)
    flux_x, flux_y = plane_fluxes(rho_ref, mom_ref, energy_ref)
    results = field_tendency(count, wx_ref[...], own_ref[...], flux_x, flux_y, late)
    for f, pieces in zip(late, results):
        corr = correction(f)
        for b, piece in enumerate(pieces):
            out_ref[f, 0, :, b * WIDTH : (b + 1) * WIDTH] = piece - corr[:, b * WIDTH : (b + 1) * WIDTH]


def exchange_plan(groups, shift_list):
    assert groups % 4 == 0 and groups >= 8
    assert sorted(shift_list) == sorted({1, 2, groups - 2, groups - 1})
    plans = []
    for step, phase in ((1, 0), (1, 1), (2, 0), (2, 1)):
        perm = []
        for r in range(groups):
            if (r // step) % 2 == phase:
                up = (r + step) % groups
                assert (up // step) % 2 != phase
                perm += [(r, up), (up, r)]
        plans.append((step, phase, step, groups - step, perm))
    return plans


def full_spec(shape):
    return pl.BlockSpec(shape, lambda z: (0,) * len(shape))


def make_local(groups):
    def local(density, momentum, energy):
        planes, rows, count = density.shape
        own, shifts = y_operator(rows, groups)
        weights = np.concatenate([w for _, _, w in shifts], axis=0)
        splits = []
        lo = 0
        for _, _, w in shifts:
            splits.append((lo, lo + w.shape[0]))
            lo += w.shape[0]
        plane_specs = [
            pl.BlockSpec((1, rows, count), lambda z: (z, 0, 0)),
            pl.BlockSpec((3, 1, rows, count), lambda z: (0, z, 0, 0)),
            pl.BlockSpec((1, rows, count), lambda z: (z, 0, 0)),
        ]
        by_shift = {e: (q, split) for (e, q, _), split in zip(shifts, splits)}
        plan = exchange_plan(groups, [e for e, _, _ in shifts])
        index = lax.axis_index("row")
        choices = [(step, phase, first, second) for step, phase, first, second, _ in plan]
        moment_shapes = [
            jax.ShapeDtypeStruct(
                (planes, 5, by_shift[first][1][1] - by_shift[first][1][0], count), jnp.float32
            )
            for _, _, first, _ in choices
        ]
        moment_specs = [
            pl.BlockSpec((1,) + s.shape[1:], lambda z: (z, 0, 0, 0)) for s in moment_shapes
        ]
        split_of = {e: by_shift[e][1] for e in by_shift}
        messages = pl.pallas_call(
            lambda *r: moments_kernel(split_of, choices, *r),
            grid=(planes,),
            in_specs=[pl.BlockSpec(memory_space=pltpu.SMEM), full_spec(weights.shape)]
            + plane_specs,
            out_specs=moment_specs,
            out_shape=moment_shapes,
        )(index.reshape(1).astype(jnp.int32), jnp.asarray(weights), density, momentum, energy)
        received = []
        spreads = []
        for (step, phase, first, second, perm), message in zip(plan, messages):
            received.append(lax.ppermute(message, "row", perm))
            take = ((index // step) % 2 == phase).astype(jnp.float32)
            spreads.append(
                take * jnp.asarray(by_shift[first][0])
                + (1.0 - take) * jnp.asarray(by_shift[second][0])
            )
        spread = jnp.concatenate(spreads, axis=1)
        wx = block_weights(count)
        out_spec = pl.BlockSpec((5, 1, rows, count), lambda z: (0, z, 0, 0))
        out_shape = jax.ShapeDtypeStruct((5, planes, rows, count), jnp.float32)
        early, late = (0, 1, 2), (3, 4)
        partial = pl.pallas_call(
            lambda *r: local_kernel(count, early, *r),
            grid=(planes,),
            in_specs=[full_spec(wx.shape), full_spec(own.shape)] + plane_specs,
            out_specs=pl.BlockSpec((len(early), 1, rows, count), lambda z: (0, z, 0, 0)),
            out_shape=jax.ShapeDtypeStruct((len(early), planes, rows, count), jnp.float32),
        )(wx, jnp.asarray(own), density, momentum, energy)
        return pl.pallas_call(
            lambda *r: final_kernel(count, early, late, *r),
            grid=(planes,),
            in_specs=[full_spec(wx.shape), full_spec(own.shape), full_spec(spread.shape)]
            + plane_specs
            + [pl.BlockSpec((len(early), 1, rows, count), lambda z: (0, z, 0, 0))]
            + [pl.BlockSpec((1,) + r.shape[1:], lambda z: (z, 0, 0, 0)) for r in received],
            out_specs=out_spec,
            out_shape=out_shape,
        )(wx, jnp.asarray(own), spread, density, momentum, energy, partial, *received)

    return local


def solution(mesh):
    in_specs = (P("col", "row", None), P(None, "col", "row", None), P("col", "row", None))
    out_specs = P(None, "col", "row", None)
    return jax.shard_map(
        make_local(mesh.shape["row"]),
        mesh=mesh,
        in_specs=in_specs,
        out_specs=out_specs,
        check_vma=False,
    )
```

```python
import jax
import jax.numpy as jnp
import numpy as np
from jax import lax
from jax.experimental import pallas as pl
from jax.experimental.pallas import tpu as pltpu
from jax.sharding import PartitionSpec as P


def operator_column(count):
    steps = np.arange(count)
    wave = 2.0 * np.pi * steps / count
    upper = (
        17.0 / 12.0 * np.sin(wave)
        + 101.0 / 300.0 * np.sin(2.0 * wave)
        + 1.0 / 300.0 * np.sin(3.0 * wave)
    )
    lower = 1.0 + np.cos(wave) + 0.1 * np.cos(2.0 * wave)
    ratio = upper / lower
    phase = 2.0 * np.pi * (steps[:, None] * steps[None, :] % count) / count
    return -np.sum(ratio[:, None] * np.sin(phase), axis=0) / count


def operator_table(count):
    column = operator_column(count)
    steps = np.arange(count)
    offsets = (steps[None, :] - steps[:, None]) % count
    return column[offsets].astype(np.float32)


def block_weights(count):
    table = operator_table(count)
    width = 128
    w_self = table[:width, :width]
    w_prev = table[:width, width : 2 * width]
    w_next = table[width : 2 * width, :width]
    return jnp.asarray(np.concatenate([w_prev, w_self, w_next], axis=1))


def column_basis(block, tol=1e-12):
    rest = block.copy()
    basis = []
    while len(basis) < block.shape[1]:
        norms = np.sqrt(np.sum(rest * rest, axis=0))
        pick = int(np.argmax(norms))
        if norms[pick] <= tol:
            break
        vec = rest[:, pick].copy()
        for _ in range(2):
            for q in basis:
                vec = vec - np.sum(q * vec) * q
        vec = vec / np.sqrt(np.sum(vec * vec))
        basis.append(vec)
        rest = rest - vec[:, None] * np.sum(vec[:, None] * rest, axis=0)[None, :]
    return basis


def y_operator(rows, groups):
    count = rows * groups
    column = operator_column(count)
    steps = np.arange(count)
    full = column[(steps[:, None] - steps[None, :]) % count]
    own = full[:rows, :rows].astype(np.float32)
    shifts = []
    for e in range(1, groups):
        block = full[:rows, rows * e : rows * (e + 1)]
        basis = column_basis(block)
        if not basis:
            continue
        q = np.stack(basis, axis=1)
        w = np.sum(q[:, :, None] * block[:, None, :], axis=0)
        shifts.append((e, q.astype(np.float32), w.astype(np.float32)))
    return own, shifts


HI = lax.Precision.HIGHEST
WIDTH = 128


def dot(a, b):
    return jnp.dot(a, b, precision=HI, preferred_element_type=jnp.float32)


def plane_fluxes(rho_ref, mom_ref, energy_ref):
    rho = rho_ref[0]
    m_x = mom_ref[0, 0]
    m_y = mom_ref[1, 0]
    m_z = mom_ref[2, 0]
    energy = energy_ref[0]
    vel_x = m_x / rho
    vel_y = m_y / rho
    pressure = 0.4 * (energy - 0.5 * (m_x * m_x + m_y * m_y + m_z * m_z) / rho)
    enthalpy = energy + pressure
    flux_x = (m_x, m_x * vel_x + pressure, m_y * vel_x, m_z * vel_x, enthalpy * vel_x)
    flux_y = (m_y, m_x * vel_y, m_y * vel_y + pressure, m_z * vel_y, enthalpy * vel_y)
    return flux_x, flux_y


def moments_kernel(splits, choices, index_ref, weights_ref, rho_ref, mom_ref, energy_ref, *out_refs):
    _, flux_y = plane_fluxes(rho_ref, mom_ref, energy_ref)
    weights = weights_ref[...]
    index = index_ref[0]
    for f in range(5):
        moments = dot(weights, flux_y[f])
        for (step, phase, first, second), out_ref in zip(choices, out_refs):
            pick = (index // step) % 2 != phase
            lo, hi = splits[first]
            lo2, hi2 = splits[second]
            out_ref[0, f] = jnp.where(pick, moments[lo:hi], moments[lo2:hi2])


def y_kernel(count, own_ref, rho_ref, mom_ref, energy_ref, out_ref):
    _, flux_y = plane_fluxes(rho_ref, mom_ref, energy_ref)
    d_all = dot(own_ref[...], jnp.concatenate(flux_y, axis=1))
    for f in range(5):
        out_ref[f, 0] = -d_all[:, f * count : (f + 1) * count]


def x_kernel(count, wx_ref, rho_ref, mom_ref, energy_ref, out_ref):
    flux_x, _ = plane_fluxes(rho_ref, mom_ref, energy_ref)
    wx = wx_ref[...]
    nb = count // WIDTH
    for f in range(5):
        fx = flux_x[f]
        rows = fx.shape[0]
        stacked = jnp.concatenate([fx[:, b * WIDTH : (b + 1) * WIDTH] for b in range(nb)], axis=0)
        parts = dot(stacked, wx)
        for b in range(nb):
            bp = (b - 1) % nb
            bn = (b + 1) % nb
            d_x = (
                parts[bp * rows : (bp + 1) * rows, :WIDTH]
                + parts[b * rows : (b + 1) * rows, WIDTH : 2 * WIDTH]
                + parts[bn * rows : (bn + 1) * rows, 2 * WIDTH :]
            )
            out_ref[f, 0, :, b * WIDTH : (b + 1) * WIDTH] = -d_x


def exchange_plan(groups, shift_list):
    assert groups % 4 == 0 and groups >= 8
    assert sorted(shift_list) == sorted({1, 2, groups - 2, groups - 1})
    plans = []
    for step, phase in ((1, 0), (1, 1), (2, 0), (2, 1)):
        perm = []
        for r in range(groups):
            if (r // step) % 2 == phase:
                up = (r + step) % groups
                assert (up // step) % 2 != phase
                perm += [(r, up), (up, r)]
        plans.append((step, phase, step, groups - step, perm))
    return plans


def full_spec(shape):
    return pl.BlockSpec(shape, lambda z: (0,) * len(shape))


def make_local(groups):
    def local(density, momentum, energy):
        planes, rows, count = density.shape
        own, shifts = y_operator(rows, groups)
        weights = np.concatenate([w for _, _, w in shifts], axis=0)
        splits = []
        lo = 0
        for _, _, w in shifts:
            splits.append((lo, lo + w.shape[0]))
            lo += w.shape[0]
        plane_specs = [
            pl.BlockSpec((1, rows, count), lambda z: (z, 0, 0)),
            pl.BlockSpec((3, 1, rows, count), lambda z: (0, z, 0, 0)),
            pl.BlockSpec((1, rows, count), lambda z: (z, 0, 0)),
        ]
        by_shift = {e: (q, split) for (e, q, _), split in zip(shifts, splits)}
        plan = exchange_plan(groups, [e for e, _, _ in shifts])
        index = lax.axis_index("row")
        choices = [(step, phase, first, second) for step, phase, first, second, _ in plan]
        moment_shapes = [
            jax.ShapeDtypeStruct(
                (planes, 5, by_shift[first][1][1] - by_shift[first][1][0], count), jnp.float32
            )
            for _, _, first, _ in choices
        ]
        moment_specs = [
            pl.BlockSpec((1,) + s.shape[1:], lambda z: (z, 0, 0, 0)) for s in moment_shapes
        ]
        split_of = {e: by_shift[e][1] for e in by_shift}
        messages = list(pl.pallas_call(
            lambda *r: moments_kernel(split_of, choices, *r),
            grid=(planes,),
            in_specs=[pl.BlockSpec(memory_space=pltpu.SMEM), full_spec(weights.shape)]
            + plane_specs,
            out_specs=moment_specs,
            out_shape=moment_shapes,
        )(index.reshape(1).astype(jnp.int32), jnp.asarray(weights), density, momentum, energy))
        wx = block_weights(count)
        out_spec = pl.BlockSpec((5, 1, rows, count), lambda z: (0, z, 0, 0))
        out_shape = jax.ShapeDtypeStruct((5, planes, rows, count), jnp.float32)
        part_y = pl.pallas_call(
            lambda *r: y_kernel(count, *r),
            grid=(planes,),
            in_specs=[full_spec(own.shape)] + plane_specs,
            out_specs=out_spec,
            out_shape=out_shape,
        )(jnp.asarray(own), density, momentum, energy)
        late = [k for k, (step, phase, _, _, _) in enumerate(plan) if phase == 1]
        held = lax.optimization_barrier(([messages[k] for k in late], part_y, density))
        for k, message in zip(late, held[0]):
            messages[k] = message
        part_y, density_late = held[1], held[2]
        received = []
        spreads = []
        for (step, phase, first, second, perm), message in zip(plan, messages):
            received.append(lax.ppermute(message, "row", perm))
            take = ((index // step) % 2 == phase).astype(jnp.float32)
            spreads.append(
                take * jnp.asarray(by_shift[first][0])
                + (1.0 - take) * jnp.asarray(by_shift[second][0])
            )
        spread = jnp.concatenate(spreads, axis=1)
        part_x = pl.pallas_call(
            lambda *r: x_kernel(count, *r),
            grid=(planes,),
            in_specs=[full_spec(wx.shape)] + plane_specs,
            out_specs=out_spec,
            out_shape=out_shape,
        )(wx, density_late, momentum, energy)
        received = jnp.concatenate(received, axis=2)
        return part_x + part_y - jnp.einsum(
            "pr,zfrx->fzpx", spread, received, precision=HI
        )

    return local


def solution(mesh):
    in_specs = (P("col", "row", None), P(None, "col", "row", None), P("col", "row", None))
    out_specs = P(None, "col", "row", None)
    return jax.shard_map(
        make_local(mesh.shape["row"]),
        mesh=mesh,
        in_specs=in_specs,
        out_specs=out_specs,
        check_vma=False,
    )
```

```python
import jax
import jax.numpy as jnp
import numpy as np
from jax import lax
from jax.experimental import pallas as pl
from jax.experimental.pallas import tpu as pltpu
from jax.sharding import PartitionSpec as P


def operator_column(count):
    steps = np.arange(count)
    wave = 2.0 * np.pi * steps / count
    upper = (
        17.0 / 12.0 * np.sin(wave)
        + 101.0 / 300.0 * np.sin(2.0 * wave)
        + 1.0 / 300.0 * np.sin(3.0 * wave)
    )
    lower = 1.0 + np.cos(wave) + 0.1 * np.cos(2.0 * wave)
    ratio = upper / lower
    phase = 2.0 * np.pi * (steps[:, None] * steps[None, :] % count) / count
    return -np.sum(ratio[:, None] * np.sin(phase), axis=0) / count


def operator_table(count):
    column = operator_column(count)
    steps = np.arange(count)
    offsets = (steps[None, :] - steps[:, None]) % count
    return column[offsets].astype(np.float32)


def block_weights(count):
    table = operator_table(count)
    width = 128
    w_self = table[:width, :width]
    w_prev = table[:width, width : 2 * width]
    w_next = table[width : 2 * width, :width]
    return jnp.asarray(np.concatenate([w_prev, w_self, w_next], axis=1))


def column_basis(block, tol=1e-12):
    rest = block.copy()
    basis = []
    while len(basis) < block.shape[1]:
        norms = np.sqrt(np.sum(rest * rest, axis=0))
        pick = int(np.argmax(norms))
        if norms[pick] <= tol:
            break
        vec = rest[:, pick].copy()
        for _ in range(2):
            for q in basis:
                vec = vec - np.sum(q * vec) * q
        vec = vec / np.sqrt(np.sum(vec * vec))
        basis.append(vec)
        rest = rest - vec[:, None] * np.sum(vec[:, None] * rest, axis=0)[None, :]
    return basis


def y_operator(rows, groups):
    count = rows * groups
    column = operator_column(count)
    steps = np.arange(count)
    full = column[(steps[:, None] - steps[None, :]) % count]
    own = full[:rows, :rows].astype(np.float32)
    shifts = []
    for e in range(1, groups):
        block = full[:rows, rows * e : rows * (e + 1)]
        basis = column_basis(block)
        if not basis:
            continue
        q = np.stack(basis, axis=1)
        w = np.sum(q[:, :, None] * block[:, None, :], axis=0)
        shifts.append((e, q.astype(np.float32), w.astype(np.float32)))
    return own, shifts


HI = lax.Precision.HIGHEST
WIDTH = 128


def dot(a, b):
    return jnp.dot(a, b, precision=HI, preferred_element_type=jnp.float32)


def plane_fluxes(rho_ref, mom_ref, energy_ref):
    rho = rho_ref[0]
    m_x = mom_ref[0, 0]
    m_y = mom_ref[1, 0]
    m_z = mom_ref[2, 0]
    energy = energy_ref[0]
    vel_x = m_x / rho
    vel_y = m_y / rho
    pressure = 0.4 * (energy - 0.5 * (m_x * m_x + m_y * m_y + m_z * m_z) / rho)
    enthalpy = energy + pressure
    flux_x = (m_x, m_x * vel_x + pressure, m_y * vel_x, m_z * vel_x, enthalpy * vel_x)
    flux_y = (m_y, m_x * vel_y, m_y * vel_y + pressure, m_z * vel_y, enthalpy * vel_y)
    return flux_x, flux_y


def moments_kernel(splits, choices, index_ref, weights_ref, rho_ref, mom_ref, energy_ref, *out_refs):
    _, flux_y = plane_fluxes(rho_ref, mom_ref, energy_ref)
    weights = weights_ref[...]
    index = index_ref[0]
    for f in range(5):
        moments = dot(weights, flux_y[f])
        for (step, phase, first, second), out_ref in zip(choices, out_refs):
            pick = (index // step) % 2 != phase
            lo, hi = splits[first]
            lo2, hi2 = splits[second]
            out_ref[0, f] = jnp.where(pick, moments[lo:hi], moments[lo2:hi2])


def local_kernel(count, wx_ref, own_ref, rho_ref, mom_ref, energy_ref, out_ref):
    flux_x, flux_y = plane_fluxes(rho_ref, mom_ref, energy_ref)
    wx = wx_ref[...]
    own = own_ref[...]
    nb = count // WIDTH
    d_all = dot(own, jnp.concatenate(flux_y, axis=1))
    for f in range(5):
        d_y = d_all[:, f * count : (f + 1) * count]
        fx = flux_x[f]
        rows = fx.shape[0]
        stacked = jnp.concatenate([fx[:, b * WIDTH : (b + 1) * WIDTH] for b in range(nb)], axis=0)
        parts = dot(stacked, wx)
        for b in range(nb):
            bp = (b - 1) % nb
            bn = (b + 1) % nb
            d_x = (
                parts[bp * rows : (bp + 1) * rows, :WIDTH]
                + parts[b * rows : (b + 1) * rows, WIDTH : 2 * WIDTH]
                + parts[bn * rows : (bn + 1) * rows, 2 * WIDTH :]
            )
            out_ref[f, 0, :, b * WIDTH : (b + 1) * WIDTH] = -(d_x + d_y[:, b * WIDTH : (b + 1) * WIDTH])


def exchange_plan(groups, shift_list):
    assert groups % 4 == 0 and groups >= 8
    assert sorted(shift_list) == sorted({1, 2, groups - 2, groups - 1})
    plans = []
    for step, phase in ((1, 0), (1, 1), (2, 0), (2, 1)):
        perm = []
        for r in range(groups):
            if (r // step) % 2 == phase:
                up = (r + step) % groups
                assert (up // step) % 2 != phase
                perm += [(r, up), (up, r)]
        plans.append((step, phase, step, groups - step, perm))
    return plans


def correct_kernel(spread_ref, partial_ref, *refs):
    recv_refs, out_ref = refs[:-1], refs[-1]
    count = partial_ref.shape[-1]
    received = jnp.concatenate(
        [jnp.concatenate([r[0, f] for r in recv_refs], axis=0) for f in range(5)], axis=1
    )
    correction = dot(spread_ref[...], received)
    for f in range(5):
        out_ref[f, 0] = partial_ref[f, 0] - correction[:, f * count : (f + 1) * count]


def full_spec(shape):
    return pl.BlockSpec(shape, lambda z: (0,) * len(shape))


def make_local(groups):
    def local(density, momentum, energy):
        planes, rows, count = density.shape
        own, shifts = y_operator(rows, groups)
        weights = np.concatenate([w for _, _, w in shifts], axis=0)
        splits = []
        lo = 0
        for _, _, w in shifts:
            splits.append((lo, lo + w.shape[0]))
            lo += w.shape[0]
        plane_specs = [
            pl.BlockSpec((1, rows, count), lambda z: (z, 0, 0)),
            pl.BlockSpec((3, 1, rows, count), lambda z: (0, z, 0, 0)),
            pl.BlockSpec((1, rows, count), lambda z: (z, 0, 0)),
        ]
        by_shift = {e: (q, split) for (e, q, _), split in zip(shifts, splits)}
        plan = exchange_plan(groups, [e for e, _, _ in shifts])
        index = lax.axis_index("row")
        choices = [(step, phase, first, second) for step, phase, first, second, _ in plan]
        moment_shapes = [
            jax.ShapeDtypeStruct(
                (planes, 5, by_shift[first][1][1] - by_shift[first][1][0], count), jnp.float32
            )
            for _, _, first, _ in choices
        ]
        moment_specs = [
            pl.BlockSpec((1,) + s.shape[1:], lambda z: (z, 0, 0, 0)) for s in moment_shapes
        ]
        split_of = {e: by_shift[e][1] for e in by_shift}
        messages = pl.pallas_call(
            lambda *r: moments_kernel(split_of, choices, *r),
            grid=(planes,),
            in_specs=[pl.BlockSpec(memory_space=pltpu.SMEM), full_spec(weights.shape)]
            + plane_specs,
            out_specs=moment_specs,
            out_shape=moment_shapes,
        )(index.reshape(1).astype(jnp.int32), jnp.asarray(weights), density, momentum, energy)
        received = []
        spreads = []
        for (step, phase, first, second, perm), message in zip(plan, messages):
            received.append(lax.ppermute(message, "row", perm))
            take = ((index // step) % 2 == phase).astype(jnp.float32)
            spreads.append(
                take * jnp.asarray(by_shift[first][0])
                + (1.0 - take) * jnp.asarray(by_shift[second][0])
            )
        spread = jnp.concatenate(spreads, axis=1)
        wx = block_weights(count)
        out_spec = pl.BlockSpec((5, 1, rows, count), lambda z: (0, z, 0, 0))
        out_shape = jax.ShapeDtypeStruct((5, planes, rows, count), jnp.float32)
        partial = pl.pallas_call(
            lambda *r: local_kernel(count, *r),
            grid=(planes,),
            in_specs=[full_spec(wx.shape), full_spec(own.shape)] + plane_specs,
            out_specs=out_spec,
            out_shape=out_shape,
        )(wx, jnp.asarray(own), density, momentum, energy)
        return pl.pallas_call(
            correct_kernel,
            grid=(planes,),
            in_specs=[full_spec(spread.shape), out_spec]
            + [pl.BlockSpec((1,) + r.shape[1:], lambda z: (z, 0, 0, 0)) for r in received],
            out_specs=out_spec,
            out_shape=out_shape,
            input_output_aliases={1: 0},
        )(spread, partial, *received)

    return local


def solution(mesh):
    in_specs = (P("col", "row", None), P(None, "col", "row", None), P("col", "row", None))
    out_specs = P(None, "col", "row", None)
    return jax.shard_map(
        make_local(mesh.shape["row"]),
        mesh=mesh,
        in_specs=in_specs,
        out_specs=out_specs,
        check_vma=False,
    )
```

```python
import jax
import jax.numpy as jnp
import numpy as np
from jax import lax
from jax.experimental import pallas as pl
from jax.experimental.pallas import tpu as pltpu
from jax.sharding import PartitionSpec as P


def operator_column(count):
    steps = np.arange(count)
    wave = 2.0 * np.pi * steps / count
    upper = (
        17.0 / 12.0 * np.sin(wave)
        + 101.0 / 300.0 * np.sin(2.0 * wave)
        + 1.0 / 300.0 * np.sin(3.0 * wave)
    )
    lower = 1.0 + np.cos(wave) + 0.1 * np.cos(2.0 * wave)
    ratio = upper / lower
    phase = 2.0 * np.pi * (steps[:, None] * steps[None, :] % count) / count
    return -np.sum(ratio[:, None] * np.sin(phase), axis=0) / count


def operator_table(count):
    column = operator_column(count)
    steps = np.arange(count)
    offsets = (steps[None, :] - steps[:, None]) % count
    return column[offsets].astype(np.float32)


def block_weights(count):
    table = operator_table(count)
    width = 128
    w_self = table[:width, :width]
    w_prev = table[:width, width : 2 * width]
    w_next = table[width : 2 * width, :width]
    return jnp.asarray(np.concatenate([w_prev, w_self, w_next], axis=1))


def column_basis(block, tol=1e-12):
    rest = block.copy()
    basis = []
    while len(basis) < block.shape[1]:
        norms = np.sqrt(np.sum(rest * rest, axis=0))
        pick = int(np.argmax(norms))
        if norms[pick] <= tol:
            break
        vec = rest[:, pick].copy()
        for _ in range(2):
            for q in basis:
                vec = vec - np.sum(q * vec) * q
        vec = vec / np.sqrt(np.sum(vec * vec))
        basis.append(vec)
        rest = rest - vec[:, None] * np.sum(vec[:, None] * rest, axis=0)[None, :]
    return basis


def y_operator(rows, groups):
    count = rows * groups
    column = operator_column(count)
    steps = np.arange(count)
    full = column[(steps[:, None] - steps[None, :]) % count]
    own = full[:rows, :rows].astype(np.float32)
    shifts = []
    for e in range(1, groups):
        block = full[:rows, rows * e : rows * (e + 1)]
        basis = column_basis(block)
        if not basis:
            continue
        q = np.stack(basis, axis=1)
        w = np.sum(q[:, :, None] * block[:, None, :], axis=0)
        shifts.append((e, q.astype(np.float32), w.astype(np.float32)))
    return own, shifts


HI = lax.Precision.HIGHEST
WIDTH = 128


def dot(a, b):
    return jnp.dot(a, b, precision=HI, preferred_element_type=jnp.float32)


def plane_fluxes(rho_ref, mom_ref, energy_ref):
    rho = rho_ref[0]
    m_x = mom_ref[0, 0]
    m_y = mom_ref[1, 0]
    m_z = mom_ref[2, 0]
    energy = energy_ref[0]
    vel_x = m_x / rho
    vel_y = m_y / rho
    pressure = 0.4 * (energy - 0.5 * (m_x * m_x + m_y * m_y + m_z * m_z) / rho)
    enthalpy = energy + pressure
    flux_x = (m_x, m_x * vel_x + pressure, m_y * vel_x, m_z * vel_x, enthalpy * vel_x)
    flux_y = (m_y, m_x * vel_y, m_y * vel_y + pressure, m_z * vel_y, enthalpy * vel_y)
    return flux_x, flux_y


def moments_kernel(splits, choices, index_ref, weights_ref, rho_ref, mom_ref, energy_ref, *out_refs):
    _, flux_y = plane_fluxes(rho_ref, mom_ref, energy_ref)
    weights = weights_ref[...]
    index = index_ref[0]
    for f in range(5):
        moments = dot(weights, flux_y[f])
        for (step, phase, first, second), out_ref in zip(choices, out_refs):
            pick = (index // step) % 2 != phase
            lo, hi = splits[first]
            lo2, hi2 = splits[second]
            out_ref[0, f] = jnp.where(pick, moments[lo:hi], moments[lo2:hi2])


def local_kernel(count, wx_ref, own_ref, rho_ref, mom_ref, energy_ref, out_hbm, out_v, out_sem):
    flux_x, flux_y = plane_fluxes(rho_ref, mom_ref, energy_ref)
    wx = wx_ref[...]
    own = own_ref[...]
    plane = pl.ds(pl.program_id(0), 1)
    nb = count // WIDTH
    d_all = dot(own, jnp.concatenate(flux_y, axis=1))
    stores = []
    for f in range(5):
        d_y = d_all[:, f * count : (f + 1) * count]
        fx = flux_x[f]
        rows = fx.shape[0]
        stacked = jnp.concatenate([fx[:, b * WIDTH : (b + 1) * WIDTH] for b in range(nb)], axis=0)
        parts = dot(stacked, wx)
        for b in range(nb):
            bp = (b - 1) % nb
            bn = (b + 1) % nb
            d_x = (
                parts[bp * rows : (bp + 1) * rows, :WIDTH]
                + parts[b * rows : (b + 1) * rows, WIDTH : 2 * WIDTH]
                + parts[bn * rows : (bn + 1) * rows, 2 * WIDTH :]
            )
            out_v[f, 0, :, b * WIDTH : (b + 1) * WIDTH] = -(d_x + d_y[:, b * WIDTH : (b + 1) * WIDTH])
        store = pltpu.make_async_copy(out_v.at[f], out_hbm.at[f, plane], out_sem.at[f])
        store.start()
        stores.append(store)
    for store in stores:
        store.wait()


def exchange_plan(groups, shift_list):
    assert groups % 4 == 0 and groups >= 8
    assert sorted(shift_list) == sorted({1, 2, groups - 2, groups - 1})
    plans = []
    for step, phase in ((1, 0), (1, 1), (2, 0), (2, 1)):
        perm = []
        for r in range(groups):
            if (r // step) % 2 == phase:
                up = (r + step) % groups
                assert (up // step) % 2 != phase
                perm += [(r, up), (up, r)]
        plans.append((step, phase, step, groups - step, perm))
    return plans


def full_spec(shape):
    return pl.BlockSpec(shape, lambda z: (0,) * len(shape))


def make_local(groups):
    def local(density, momentum, energy):
        planes, rows, count = density.shape
        own, shifts = y_operator(rows, groups)
        weights = np.concatenate([w for _, _, w in shifts], axis=0)
        splits = []
        lo = 0
        for _, _, w in shifts:
            splits.append((lo, lo + w.shape[0]))
            lo += w.shape[0]
        plane_specs = [
            pl.BlockSpec((1, rows, count), lambda z: (z, 0, 0)),
            pl.BlockSpec((3, 1, rows, count), lambda z: (0, z, 0, 0)),
            pl.BlockSpec((1, rows, count), lambda z: (z, 0, 0)),
        ]
        by_shift = {e: (q, split) for (e, q, _), split in zip(shifts, splits)}
        plan = exchange_plan(groups, [e for e, _, _ in shifts])
        index = lax.axis_index("row")
        choices = [(step, phase, first, second) for step, phase, first, second, _ in plan]
        moment_shapes = [
            jax.ShapeDtypeStruct(
                (planes, 5, by_shift[first][1][1] - by_shift[first][1][0], count), jnp.float32
            )
            for _, _, first, _ in choices
        ]
        moment_specs = [
            pl.BlockSpec((1,) + s.shape[1:], lambda z: (z, 0, 0, 0)) for s in moment_shapes
        ]
        split_of = {e: by_shift[e][1] for e in by_shift}
        messages = pl.pallas_call(
            lambda *r: moments_kernel(split_of, choices, *r),
            grid=(planes,),
            in_specs=[pl.BlockSpec(memory_space=pltpu.SMEM), full_spec(weights.shape)]
            + plane_specs,
            out_specs=moment_specs,
            out_shape=moment_shapes,
        )(index.reshape(1).astype(jnp.int32), jnp.asarray(weights), density, momentum, energy)
        received = []
        spreads = []
        for (step, phase, first, second, perm), message in zip(plan, messages):
            received.append(lax.ppermute(message, "row", perm))
            take = ((index // step) % 2 == phase).astype(jnp.float32)
            spreads.append(
                take * jnp.asarray(by_shift[first][0])
                + (1.0 - take) * jnp.asarray(by_shift[second][0])
            )
        spread = jnp.concatenate(spreads, axis=1)
        wx = block_weights(count)
        out_spec = pl.BlockSpec((5, 1, rows, count), lambda z: (0, z, 0, 0))
        out_shape = jax.ShapeDtypeStruct((5, planes, rows, count), jnp.float32)
        partial = pl.pallas_call(
            lambda *r: local_kernel(count, *r),
            grid=(planes,),
            in_specs=[full_spec(wx.shape), full_spec(own.shape)] + plane_specs,
            out_specs=pl.BlockSpec(memory_space=pl.ANY),
            out_shape=out_shape,
            scratch_shapes=[
                pltpu.VMEM((5, 1, rows, count), jnp.float32),
                pltpu.SemaphoreType.DMA((5,)),
            ],
        )(wx, jnp.asarray(own), density, momentum, energy)
        received = jnp.concatenate(received, axis=2)
        return partial - jnp.einsum(
            "pr,zfrx->fzpx", spread, received, precision=HI
        )

    return local


def solution(mesh):
    in_specs = (P("col", "row", None), P(None, "col", "row", None), P("col", "row", None))
    out_specs = P(None, "col", "row", None)
    return jax.shard_map(
        make_local(mesh.shape["row"]),
        mesh=mesh,
        in_specs=in_specs,
        out_specs=out_specs,
        check_vma=False,
    )
```

```python
import jax
import jax.numpy as jnp
import numpy as np
from jax import lax
from jax.experimental import pallas as pl
from jax.experimental.pallas import tpu as pltpu
from jax.sharding import PartitionSpec as P


def operator_column(count):
    steps = np.arange(count)
    wave = 2.0 * np.pi * steps / count
    upper = (
        17.0 / 12.0 * np.sin(wave)
        + 101.0 / 300.0 * np.sin(2.0 * wave)
        + 1.0 / 300.0 * np.sin(3.0 * wave)
    )
    lower = 1.0 + np.cos(wave) + 0.1 * np.cos(2.0 * wave)
    ratio = upper / lower
    phase = 2.0 * np.pi * (steps[:, None] * steps[None, :] % count) / count
    return -np.sum(ratio[:, None] * np.sin(phase), axis=0) / count


def operator_table(count):
    column = operator_column(count)
    steps = np.arange(count)
    offsets = (steps[None, :] - steps[:, None]) % count
    return column[offsets].astype(np.float32)


def block_weights(count):
    table = operator_table(count)
    width = 128
    w_self = table[:width, :width]
    w_prev = table[:width, width : 2 * width]
    w_next = table[width : 2 * width, :width]
    return jnp.asarray(np.concatenate([w_prev, w_self, w_next], axis=1))


def column_basis(block, tol=1e-12):
    rest = block.copy()
    basis = []
    while len(basis) < block.shape[1]:
        norms = np.sqrt(np.sum(rest * rest, axis=0))
        pick = int(np.argmax(norms))
        if norms[pick] <= tol:
            break
        vec = rest[:, pick].copy()
        for _ in range(2):
            for q in basis:
                vec = vec - np.sum(q * vec) * q
        vec = vec / np.sqrt(np.sum(vec * vec))
        basis.append(vec)
        rest = rest - vec[:, None] * np.sum(vec[:, None] * rest, axis=0)[None, :]
    return basis


def y_operator(rows, groups):
    count = rows * groups
    column = operator_column(count)
    steps = np.arange(count)
    full = column[(steps[:, None] - steps[None, :]) % count]
    own = full[:rows, :rows].astype(np.float32)
    shifts = []
    for e in range(1, groups):
        block = full[:rows, rows * e : rows * (e + 1)]
        basis = column_basis(block)
        if not basis:
            continue
        q = np.stack(basis, axis=1)
        w = np.sum(q[:, :, None] * block[:, None, :], axis=0)
        shifts.append((e, q.astype(np.float32), w.astype(np.float32)))
    return own, shifts


HI = lax.Precision.HIGHEST
WIDTH = 128


def dot(a, b):
    return jnp.dot(a, b, precision=HI, preferred_element_type=jnp.float32)


def plane_fluxes(rho_ref, mom_ref, energy_ref):
    rho = rho_ref[0]
    m_x = mom_ref[0, 0]
    m_y = mom_ref[1, 0]
    m_z = mom_ref[2, 0]
    energy = energy_ref[0]
    vel_x = m_x / rho
    vel_y = m_y / rho
    pressure = 0.4 * (energy - 0.5 * (m_x * m_x + m_y * m_y + m_z * m_z) / rho)
    enthalpy = energy + pressure
    flux_x = (m_x, m_x * vel_x + pressure, m_y * vel_x, m_z * vel_x, enthalpy * vel_x)
    flux_y = (m_y, m_x * vel_y, m_y * vel_y + pressure, m_z * vel_y, enthalpy * vel_y)
    return flux_x, flux_y


def side(r, step):
    return (r // step + (r % 2 if step == 2 else 0)) % 2


def moments_kernel(splits, choices, index_ref, weights_ref, rho_ref, mom_ref, energy_ref, *out_refs):
    _, flux_y = plane_fluxes(rho_ref, mom_ref, energy_ref)
    weights = weights_ref[...]
    index = index_ref[0]
    for f in range(5):
        moments = dot(weights, flux_y[f])
        for (step, phase, first, second), out_ref in zip(choices, out_refs):
            pick = side(index, step) != phase
            lo, hi = splits[first]
            lo2, hi2 = splits[second]
            out_ref[0, f] = jnp.where(pick, moments[lo:hi], moments[lo2:hi2])


def local_kernel(count, wx_ref, own_ref, rho_ref, mom_ref, energy_ref, out_ref):
    flux_x, flux_y = plane_fluxes(rho_ref, mom_ref, energy_ref)
    wx = wx_ref[...]
    own = own_ref[...]
    nb = count // WIDTH
    d_all = dot(own, jnp.concatenate(flux_y, axis=1))
    for f in range(5):
        d_y = d_all[:, f * count : (f + 1) * count]
        fx = flux_x[f]
        rows = fx.shape[0]
        stacked = jnp.concatenate([fx[:, b * WIDTH : (b + 1) * WIDTH] for b in range(nb)], axis=0)
        parts = dot(stacked, wx)
        for b in range(nb):
            bp = (b - 1) % nb
            bn = (b + 1) % nb
            d_x = (
                parts[bp * rows : (bp + 1) * rows, :WIDTH]
                + parts[b * rows : (b + 1) * rows, WIDTH : 2 * WIDTH]
                + parts[bn * rows : (bn + 1) * rows, 2 * WIDTH :]
            )
            out_ref[f, 0, :, b * WIDTH : (b + 1) * WIDTH] = -(d_x + d_y[:, b * WIDTH : (b + 1) * WIDTH])


def exchange_plan(groups, shift_list):
    assert groups % 4 == 0 and groups >= 8
    assert sorted(shift_list) == sorted({1, 2, groups - 2, groups - 1})
    plans = []
    for step, phase in ((1, 0), (1, 1), (2, 0), (2, 1)):
        perm = []
        for r in range(groups):
            if side(r, step) == phase:
                up = (r + step) % groups
                assert side(up, step) != phase
                perm += [(r, up), (up, r)]
        plans.append((step, phase, step, groups - step, perm))
    return plans


def full_spec(shape):
    return pl.BlockSpec(shape, lambda z: (0,) * len(shape))


def make_local(groups):
    def local(density, momentum, energy):
        planes, rows, count = density.shape
        own, shifts = y_operator(rows, groups)
        weights = np.concatenate([w for _, _, w in shifts], axis=0)
        splits = []
        lo = 0
        for _, _, w in shifts:
            splits.append((lo, lo + w.shape[0]))
            lo += w.shape[0]
        plane_specs = [
            pl.BlockSpec((1, rows, count), lambda z: (z, 0, 0)),
            pl.BlockSpec((3, 1, rows, count), lambda z: (0, z, 0, 0)),
            pl.BlockSpec((1, rows, count), lambda z: (z, 0, 0)),
        ]
        by_shift = {e: (q, split) for (e, q, _), split in zip(shifts, splits)}
        plan = exchange_plan(groups, [e for e, _, _ in shifts])
        index = lax.axis_index("row")
        choices = [(step, phase, first, second) for step, phase, first, second, _ in plan]
        moment_shapes = [
            jax.ShapeDtypeStruct(
                (planes, 5, by_shift[first][1][1] - by_shift[first][1][0], count), jnp.float32
            )
            for _, _, first, _ in choices
        ]
        moment_specs = [
            pl.BlockSpec((1,) + s.shape[1:], lambda z: (z, 0, 0, 0)) for s in moment_shapes
        ]
        split_of = {e: by_shift[e][1] for e in by_shift}
        messages = pl.pallas_call(
            lambda *r: moments_kernel(split_of, choices, *r),
            grid=(planes,),
            in_specs=[pl.BlockSpec(memory_space=pltpu.SMEM), full_spec(weights.shape)]
            + plane_specs,
            out_specs=moment_specs,
            out_shape=moment_shapes,
        )(index.reshape(1).astype(jnp.int32), jnp.asarray(weights), density, momentum, energy)
        received = []
        spreads = []
        for (step, phase, first, second, perm), message in zip(plan, messages):
            received.append(lax.ppermute(message, "row", perm))
            take = (side(index, step) == phase).astype(jnp.float32)
            spreads.append(
                take * jnp.asarray(by_shift[first][0])
                + (1.0 - take) * jnp.asarray(by_shift[second][0])
            )
        spread = jnp.concatenate(spreads, axis=1)
        wx = block_weights(count)
        out_spec = pl.BlockSpec((5, 1, rows, count), lambda z: (0, z, 0, 0))
        out_shape = jax.ShapeDtypeStruct((5, planes, rows, count), jnp.float32)
        partial = pl.pallas_call(
            lambda *r: local_kernel(count, *r),
            grid=(planes,),
            in_specs=[full_spec(wx.shape), full_spec(own.shape)] + plane_specs,
            out_specs=out_spec,
            out_shape=out_shape,
        )(wx, jnp.asarray(own), density, momentum, energy)
        received = jnp.concatenate(received, axis=2)
        return partial - jnp.einsum(
            "pr,zfrx->fzpx", spread, received, precision=HI
        )

    return local


def solution(mesh):
    in_specs = (P("col", "row", None), P(None, "col", "row", None), P("col", "row", None))
    out_specs = P(None, "col", "row", None)
    return jax.shard_map(
        make_local(mesh.shape["row"]),
        mesh=mesh,
        in_specs=in_specs,
        out_specs=out_specs,
        check_vma=False,
    )
```

```python
import jax
import jax.numpy as jnp
import numpy as np
from jax import lax
from jax.experimental import pallas as pl
from jax.experimental.pallas import tpu as pltpu
from jax.sharding import PartitionSpec as P


def operator_column(count):
    steps = np.arange(count)
    wave = 2.0 * np.pi * steps / count
    upper = (
        17.0 / 12.0 * np.sin(wave)
        + 101.0 / 300.0 * np.sin(2.0 * wave)
        + 1.0 / 300.0 * np.sin(3.0 * wave)
    )
    lower = 1.0 + np.cos(wave) + 0.1 * np.cos(2.0 * wave)
    ratio = upper / lower
    phase = 2.0 * np.pi * (steps[:, None] * steps[None, :] % count) / count
    return -np.sum(ratio[:, None] * np.sin(phase), axis=0) / count


def operator_table(count):
    column = operator_column(count)
    steps = np.arange(count)
    offsets = (steps[None, :] - steps[:, None]) % count
    return column[offsets].astype(np.float32)


def block_weights(count):
    table = operator_table(count)
    width = 128
    w_self = table[:width, :width]
    w_prev = table[:width, width : 2 * width]
    w_next = table[width : 2 * width, :width]
    return jnp.asarray(np.concatenate([w_prev, w_self, w_next], axis=1))


def column_basis(block, tol=1e-12):
    rest = block.copy()
    basis = []
    while len(basis) < block.shape[1]:
        norms = np.sqrt(np.sum(rest * rest, axis=0))
        pick = int(np.argmax(norms))
        if norms[pick] <= tol:
            break
        vec = rest[:, pick].copy()
        for _ in range(2):
            for q in basis:
                vec = vec - np.sum(q * vec) * q
        vec = vec / np.sqrt(np.sum(vec * vec))
        basis.append(vec)
        rest = rest - vec[:, None] * np.sum(vec[:, None] * rest, axis=0)[None, :]
    return basis


def y_operator(rows, groups):
    count = rows * groups
    column = operator_column(count)
    steps = np.arange(count)
    full = column[(steps[:, None] - steps[None, :]) % count]
    own = full[:rows, :rows].astype(np.float32)
    shifts = []
    for e in range(1, groups):
        block = full[:rows, rows * e : rows * (e + 1)]
        basis = column_basis(block)
        if not basis:
            continue
        q = np.stack(basis, axis=1)
        w = np.sum(q[:, :, None] * block[:, None, :], axis=0)
        shifts.append((e, q.astype(np.float32), w.astype(np.float32)))
    return own, shifts


HI = lax.Precision.HIGHEST
WIDTH = 128


def dot(a, b):
    return jnp.dot(a, b, precision=HI, preferred_element_type=jnp.float32)


def plane_fluxes(rho_ref, mom_ref, energy_ref):
    rho = rho_ref[0]
    m_x = mom_ref[0, 0]
    m_y = mom_ref[1, 0]
    m_z = mom_ref[2, 0]
    energy = energy_ref[0]
    vel_x = m_x / rho
    vel_y = m_y / rho
    pressure = 0.4 * (energy - 0.5 * (m_x * m_x + m_y * m_y + m_z * m_z) / rho)
    enthalpy = energy + pressure
    flux_x = (m_x, m_x * vel_x + pressure, m_y * vel_x, m_z * vel_x, enthalpy * vel_x)
    flux_y = (m_y, m_x * vel_y, m_y * vel_y + pressure, m_z * vel_y, enthalpy * vel_y)
    return flux_x, flux_y


def side(r, step):
    return (r // step + (r % 2 if step == 2 else 0)) % 2


def moments_kernel(splits, choices, index_ref, weights_ref, rho_ref, mom_ref, energy_ref, *out_refs):
    _, flux_y = plane_fluxes(rho_ref, mom_ref, energy_ref)
    weights = weights_ref[...]
    index = index_ref[0]
    for f in range(5):
        moments = dot(weights, flux_y[f])
        for (step, phase, first, second), out_ref in zip(choices, out_refs):
            pick = side(index, step) != phase
            lo, hi = splits[first]
            lo2, hi2 = splits[second]
            out_ref[0, f] = jnp.where(pick, moments[lo:hi], moments[lo2:hi2])


def local_kernel(count, wx_ref, own_ref, rho_ref, mom_ref, energy_ref, out_hbm, out_v, out_sem):
    flux_x, flux_y = plane_fluxes(rho_ref, mom_ref, energy_ref)
    wx = wx_ref[...]
    own = own_ref[...]
    plane = pl.ds(pl.program_id(0), 1)
    nb = count // WIDTH
    d_all = dot(own, jnp.concatenate(flux_y, axis=1))
    stores = []
    for f in range(5):
        d_y = d_all[:, f * count : (f + 1) * count]
        fx = flux_x[f]
        rows = fx.shape[0]
        stacked = jnp.concatenate([fx[:, b * WIDTH : (b + 1) * WIDTH] for b in range(nb)], axis=0)
        parts = dot(stacked, wx)
        for b in range(nb):
            bp = (b - 1) % nb
            bn = (b + 1) % nb
            d_x = (
                parts[bp * rows : (bp + 1) * rows, :WIDTH]
                + parts[b * rows : (b + 1) * rows, WIDTH : 2 * WIDTH]
                + parts[bn * rows : (bn + 1) * rows, 2 * WIDTH :]
            )
            out_v[f, 0, :, b * WIDTH : (b + 1) * WIDTH] = -(d_x + d_y[:, b * WIDTH : (b + 1) * WIDTH])
        store = pltpu.make_async_copy(out_v.at[f], out_hbm.at[f, plane], out_sem.at[f])
        store.start()
        stores.append(store)
    for store in stores:
        store.wait()


def exchange_plan(groups, shift_list):
    assert groups % 4 == 0 and groups >= 8
    assert sorted(shift_list) == sorted({1, 2, groups - 2, groups - 1})
    plans = []
    for step, phase in ((1, 0), (1, 1), (2, 0), (2, 1)):
        perm = []
        for r in range(groups):
            if side(r, step) == phase:
                up = (r + step) % groups
                assert side(up, step) != phase
                perm += [(r, up), (up, r)]
        plans.append((step, phase, step, groups - step, perm))
    return plans


def full_spec(shape):
    return pl.BlockSpec(shape, lambda z: (0,) * len(shape))


def make_local(groups):
    def local(density, momentum, energy):
        planes, rows, count = density.shape
        own, shifts = y_operator(rows, groups)
        weights = np.concatenate([w for _, _, w in shifts], axis=0)
        splits = []
        lo = 0
        for _, _, w in shifts:
            splits.append((lo, lo + w.shape[0]))
            lo += w.shape[0]
        plane_specs = [
            pl.BlockSpec((1, rows, count), lambda z: (z, 0, 0)),
            pl.BlockSpec((3, 1, rows, count), lambda z: (0, z, 0, 0)),
            pl.BlockSpec((1, rows, count), lambda z: (z, 0, 0)),
        ]
        by_shift = {e: (q, split) for (e, q, _), split in zip(shifts, splits)}
        plan = exchange_plan(groups, [e for e, _, _ in shifts])
        index = lax.axis_index("row")
        choices = [(step, phase, first, second) for step, phase, first, second, _ in plan]
        moment_shapes = [
            jax.ShapeDtypeStruct(
                (planes, 5, by_shift[first][1][1] - by_shift[first][1][0], count), jnp.float32
            )
            for _, _, first, _ in choices
        ]
        moment_specs = [
            pl.BlockSpec((1,) + s.shape[1:], lambda z: (z, 0, 0, 0)) for s in moment_shapes
        ]
        split_of = {e: by_shift[e][1] for e in by_shift}
        messages = pl.pallas_call(
            lambda *r: moments_kernel(split_of, choices, *r),
            grid=(planes,),
            in_specs=[pl.BlockSpec(memory_space=pltpu.SMEM), full_spec(weights.shape)]
            + plane_specs,
            out_specs=moment_specs,
            out_shape=moment_shapes,
        )(index.reshape(1).astype(jnp.int32), jnp.asarray(weights), density, momentum, energy)
        received = []
        spreads = []
        for (step, phase, first, second, perm), message in zip(plan, messages):
            received.append(lax.ppermute(message, "row", perm))
            take = (side(index, step) == phase).astype(jnp.float32)
            spreads.append(
                take * jnp.asarray(by_shift[first][0])
                + (1.0 - take) * jnp.asarray(by_shift[second][0])
            )
        spread = jnp.concatenate(spreads, axis=1)
        wx = block_weights(count)
        out_spec = pl.BlockSpec((5, 1, rows, count), lambda z: (0, z, 0, 0))
        out_shape = jax.ShapeDtypeStruct((5, planes, rows, count), jnp.float32)
        partial = pl.pallas_call(
            lambda *r: local_kernel(count, *r),
            grid=(planes,),
            in_specs=[full_spec(wx.shape), full_spec(own.shape)] + plane_specs,
            out_specs=pl.BlockSpec(memory_space=pl.ANY),
            out_shape=out_shape,
            scratch_shapes=[
                pltpu.VMEM((5, 1, rows, count), jnp.float32),
                pltpu.SemaphoreType.DMA((5,)),
            ],
        )(wx, jnp.asarray(own), density, momentum, energy)
        received = jnp.concatenate(received, axis=2)
        return partial - jnp.einsum(
            "pr,zfrx->fzpx", spread, received, precision=HI
        )

    return local


def solution(mesh):
    in_specs = (P("col", "row", None), P(None, "col", "row", None), P("col", "row", None))
    out_specs = P(None, "col", "row", None)
    return jax.shard_map(
        make_local(mesh.shape["row"]),
        mesh=mesh,
        in_specs=in_specs,
        out_specs=out_specs,
        check_vma=False,
    )
```

```python
import jax
import jax.numpy as jnp
import numpy as np
from jax import lax
from jax.experimental import pallas as pl
from jax.experimental.pallas import tpu as pltpu
from jax.sharding import PartitionSpec as P


def operator_column(count):
    steps = np.arange(count)
    wave = 2.0 * np.pi * steps / count
    upper = (
        17.0 / 12.0 * np.sin(wave)
        + 101.0 / 300.0 * np.sin(2.0 * wave)
        + 1.0 / 300.0 * np.sin(3.0 * wave)
    )
    lower = 1.0 + np.cos(wave) + 0.1 * np.cos(2.0 * wave)
    ratio = upper / lower
    phase = 2.0 * np.pi * (steps[:, None] * steps[None, :] % count) / count
    return -np.sum(ratio[:, None] * np.sin(phase), axis=0) / count


def operator_table(count):
    column = operator_column(count)
    steps = np.arange(count)
    offsets = (steps[None, :] - steps[:, None]) % count
    return column[offsets].astype(np.float32)


def block_weights(count):
    table = operator_table(count)
    width = 128
    w_self = table[:width, :width]
    w_prev = table[:width, width : 2 * width]
    w_next = table[width : 2 * width, :width]
    return jnp.asarray(np.concatenate([w_prev, w_self, w_next], axis=1))


def column_basis(block, tol=1e-12):
    rest = block.copy()
    basis = []
    while len(basis) < block.shape[1]:
        norms = np.sqrt(np.sum(rest * rest, axis=0))
        pick = int(np.argmax(norms))
        if norms[pick] <= tol:
            break
        vec = rest[:, pick].copy()
        for _ in range(2):
            for q in basis:
                vec = vec - np.sum(q * vec) * q
        vec = vec / np.sqrt(np.sum(vec * vec))
        basis.append(vec)
        rest = rest - vec[:, None] * np.sum(vec[:, None] * rest, axis=0)[None, :]
    return basis


def y_operator(rows, groups):
    count = rows * groups
    column = operator_column(count)
    steps = np.arange(count)
    full = column[(steps[:, None] - steps[None, :]) % count]
    own = full[:rows, :rows].astype(np.float32)
    shifts = []
    for e in range(1, groups):
        block = full[:rows, rows * e : rows * (e + 1)]
        basis = column_basis(block)
        if not basis:
            continue
        q = np.stack(basis, axis=1)
        w = np.sum(q[:, :, None] * block[:, None, :], axis=0)
        shifts.append((e, q.astype(np.float32), w.astype(np.float32)))
    return own, shifts


HI = lax.Precision.HIGHEST
WIDTH = 128


def dot(a, b):
    return jnp.dot(a, b, precision=HI, preferred_element_type=jnp.float32)


def plane_fluxes(rho_ref, mom_ref, energy_ref):
    rho = rho_ref[0]
    m_x = mom_ref[0, 0]
    m_y = mom_ref[1, 0]
    m_z = mom_ref[2, 0]
    energy = energy_ref[0]
    vel_x = m_x / rho
    vel_y = m_y / rho
    pressure = 0.4 * (energy - 0.5 * (m_x * m_x + m_y * m_y + m_z * m_z) / rho)
    enthalpy = energy + pressure
    flux_x = (m_x, m_x * vel_x + pressure, m_y * vel_x, m_z * vel_x, enthalpy * vel_x)
    flux_y = (m_y, m_x * vel_y, m_y * vel_y + pressure, m_z * vel_y, enthalpy * vel_y)
    return flux_x, flux_y


def side(r, step):
    return (r // step + (r % 2 if step == 2 else 0)) % 2


def moments_kernel(splits, choices, index_ref, weights_ref, rho_ref, mom_ref, energy_ref, *out_refs):
    _, flux_y = plane_fluxes(rho_ref, mom_ref, energy_ref)
    weights = weights_ref[...]
    index = index_ref[0]
    for f in range(5):
        moments = dot(weights, flux_y[f])
        for (step, phase, first, second), out_ref in zip(choices, out_refs):
            pick = side(index, step) != phase
            lo, hi = splits[first]
            lo2, hi2 = splits[second]
            out_ref[0, f] = jnp.where(pick, moments[lo:hi], moments[lo2:hi2])


def local_kernel(count, wx_ref, own_ref, rho_ref, mom_ref, energy_ref, out_hbm, out_v, out_sem):
    flux_x, flux_y = plane_fluxes(rho_ref, mom_ref, energy_ref)
    wx = wx_ref[...]
    own = own_ref[...]
    plane = pl.ds(pl.program_id(0), 1)
    nb = count // WIDTH
    d_all = dot(own, jnp.concatenate(flux_y, axis=1))
    stores = []
    for f in range(5):
        d_y = d_all[:, f * count : (f + 1) * count]
        fx = flux_x[f]
        rows = fx.shape[0]
        stacked = jnp.concatenate([fx[:, b * WIDTH : (b + 1) * WIDTH] for b in range(nb)], axis=0)
        parts = dot(stacked, wx)
        for b in range(nb):
            bp = (b - 1) % nb
            bn = (b + 1) % nb
            d_x = (
                parts[bp * rows : (bp + 1) * rows, :WIDTH]
                + parts[b * rows : (b + 1) * rows, WIDTH : 2 * WIDTH]
                + parts[bn * rows : (bn + 1) * rows, 2 * WIDTH :]
            )
            out_v[f, 0, :, b * WIDTH : (b + 1) * WIDTH] = -(d_x + d_y[:, b * WIDTH : (b + 1) * WIDTH])
        store = pltpu.make_async_copy(out_v.at[f], out_hbm.at[f, plane], out_sem.at[f])
        store.start()
        stores.append(store)
    for store in stores:
        store.wait()


def exchange_plan(groups, shift_list):
    assert groups % 4 == 0 and groups >= 8
    assert sorted(shift_list) == sorted({1, 2, groups - 2, groups - 1})
    plans = []
    for step, phase in ((1, 0), (1, 1), (2, 0), (2, 1)):
        perm = []
        for r in range(groups):
            if side(r, step) == phase:
                up = (r + step) % groups
                assert side(up, step) != phase
                perm += [(r, up), (up, r)]
        plans.append((step, phase, step, groups - step, perm))
    return plans


def full_spec(shape):
    return pl.BlockSpec(shape, lambda z: (0,) * len(shape))


def make_local(groups):
    def local(density, momentum, energy):
        planes, rows, count = density.shape
        own, shifts = y_operator(rows, groups)
        weights = np.concatenate([w for _, _, w in shifts], axis=0)
        splits = []
        lo = 0
        for _, _, w in shifts:
            splits.append((lo, lo + w.shape[0]))
            lo += w.shape[0]
        plane_specs = [
            pl.BlockSpec((1, rows, count), lambda z: (z, 0, 0)),
            pl.BlockSpec((3, 1, rows, count), lambda z: (0, z, 0, 0)),
            pl.BlockSpec((1, rows, count), lambda z: (z, 0, 0)),
        ]
        by_shift = {e: (q, split) for (e, q, _), split in zip(shifts, splits)}
        plan = exchange_plan(groups, [e for e, _, _ in shifts])
        index = lax.axis_index("row")
        choices = [(step, phase, first, second) for step, phase, first, second, _ in plan]
        moment_shapes = [
            jax.ShapeDtypeStruct(
                (planes, 5, by_shift[first][1][1] - by_shift[first][1][0], count), jnp.float32
            )
            for _, _, first, _ in choices
        ]
        moment_specs = [
            pl.BlockSpec((1,) + s.shape[1:], lambda z: (z, 0, 0, 0)) for s in moment_shapes
        ]
        split_of = {e: by_shift[e][1] for e in by_shift}
        messages = pl.pallas_call(
            lambda *r: moments_kernel(split_of, choices, *r),
            grid=(planes,),
            in_specs=[pl.BlockSpec(memory_space=pltpu.SMEM), full_spec(weights.shape)]
            + plane_specs,
            out_specs=moment_specs,
            out_shape=moment_shapes,
        )(index.reshape(1).astype(jnp.int32), jnp.asarray(weights), density, momentum, energy)
        received = []
        spreads = []
        for (step, phase, first, second, perm), message in zip(plan, messages):
            received.append(lax.ppermute(message, "row", perm))
            take = (side(index, step) == phase).astype(jnp.float32)
            spreads.append(
                take * jnp.asarray(by_shift[first][0])
                + (1.0 - take) * jnp.asarray(by_shift[second][0])
            )
        spread = jnp.concatenate(spreads, axis=1)
        wx = block_weights(count)
        out_spec = pl.BlockSpec((5, 1, rows, count), lambda z: (0, z, 0, 0))
        out_shape = jax.ShapeDtypeStruct((5, planes, rows, count), jnp.float32)
        partial = pl.pallas_call(
            lambda *r: local_kernel(count, *r),
            grid=(planes,),
            in_specs=[full_spec(wx.shape), full_spec(own.shape)] + plane_specs,
            out_specs=pl.BlockSpec(memory_space=pl.ANY),
            out_shape=out_shape,
            scratch_shapes=[
                pltpu.VMEM((5, 1, rows, count), jnp.float32),
                pltpu.SemaphoreType.DMA((5,)),
            ],
        )(wx, jnp.asarray(own), density, momentum, energy)
        received = jnp.concatenate(received, axis=2)
        out = partial
        for r in range(received.shape[2]):
            out = out - spread[None, None, :, r : r + 1] * jnp.moveaxis(received[:, :, r : r + 1, :], 1, 0)
        return out

    return local


def solution(mesh):
    in_specs = (P("col", "row", None), P(None, "col", "row", None), P("col", "row", None))
    out_specs = P(None, "col", "row", None)
    return jax.shard_map(
        make_local(mesh.shape["row"]),
        mesh=mesh,
        in_specs=in_specs,
        out_specs=out_specs,
        check_vma=False,
    )
```
